512 devices in a mesh: section: 8 (over x, core), dp: 64 (over y, z).
Axes of the slice: x: 4, y: 4, z: 16, core: 2. Of those that a mesh axis runs over, the one named last changes fastest.
Arguments:
- activations: bfloat16 [8, 8192, 5120], P('section', 'dp'), may hold values from -200 to 200, as said below
- upstream: bfloat16 [8, 8192, 5120], P('section', 'dp'), may hold values from -120 to 120, as said below
- section_norm_gain: float32 [8, 5120], P('section'), may hold values from 0.1 to 1.9
- adapter_down_weight: bfloat16 [8, 16, 5120], P('section'), may hold values from -0.078125 to 0.078125
- adapter_up_weight: bfloat16 [8, 16, 5120], P('section'), may hold values from -0.078125 to 0.078125
Outputs:
- passed: bfloat16 [8, 8192, 5120], P('section', 'dp')
- grad_pair: bfloat16 [8, 163840], P('section', 'dp')
The draws below stay inside these ranges and needn't reach their ends.
Inputs may be any that keep to these rules, and one draw needn't show every extreme that they name: `activations`: activations of one token position share a part across replicas; rows and features have different scales. `upstream`: gradients of one token position share a part across replicas.
All inputs are finite; a program needn't handle non-finite values.
Results may differ from the reference program's by a relative error of at most 0.0034.
Values may be sent and summed in bfloat16 or wider, within the bound.
No kernel may reach another device: no remote copies, remote signals or barrier semaphores. Data moves between devices by JAX's collectives and lax.ppermute only.
A program may use at most 64 MiB of HBM per device.

```python
import math
import jax
import jax.numpy as jnp
from jax import lax

MODEL_WIDTH = 5120
ADAPTER_RANK = 16
TOK_DEV = 128
RELAY_SECTIONS = 8
REPLICAS = 64
ROWS = 8192
LEVELS = 6


def draw_activations(key, part):
    subkeys = jax.random.split(key, 4)
    shared = jnp.clip(jax.random.normal(subkeys[0], (RELAY_SECTIONS, 1, TOK_DEV, MODEL_WIDTH)), -4.0, 4.0)
    private = jnp.clip(jax.random.normal(subkeys[1], (RELAY_SECTIONS, REPLICAS, TOK_DEV, MODEL_WIDTH)), -4.0, 4.0)
    mixture = 0.75 * shared + 0.66 * private
    row_scale = jnp.exp(jax.random.uniform(subkeys[2], (RELAY_SECTIONS, REPLICAS, TOK_DEV, 1), minval=0.0, maxval=math.log(10.0)))
    column_scale = jnp.exp(jax.random.uniform(subkeys[3], (RELAY_SECTIONS, 1, 1, MODEL_WIDTH), minval=0.0, maxval=math.log(10.0)))
    values = mixture * row_scale * column_scale / 3.0
    return values.reshape(RELAY_SECTIONS, ROWS, MODEL_WIDTH).astype(jnp.bfloat16)


def draw_upstream(key, part):
    subkeys = jax.random.split(key, 3)
    shared = jnp.clip(jax.random.normal(subkeys[0], (RELAY_SECTIONS, 1, TOK_DEV, MODEL_WIDTH)), -4.0, 4.0)
    private = jnp.clip(jax.random.normal(subkeys[1], (RELAY_SECTIONS, REPLICAS, TOK_DEV, MODEL_WIDTH)), -4.0, 4.0)
    ramp_scale = 1.0 + 2.0 * jnp.arange(REPLICAS, dtype=jnp.float32).reshape(1, REPLICAS, 1, 1) / (REPLICAS - 1)
    row_scale = jnp.exp(jax.random.uniform(subkeys[2], (RELAY_SECTIONS, REPLICAS, TOK_DEV, 1), minval=0.0, maxval=math.log(2.0)))
    values = (0.75 * shared + 0.66 * private) * ramp_scale * row_scale
    return values.reshape(RELAY_SECTIONS, ROWS, MODEL_WIDTH).astype(jnp.bfloat16)


def levels(stream_key, extent, pieces, smallest, top_value):
    loudness, own = 1.0, jax.random.fold_in(stream_key, 6)
    for dim, parts in pieces:
        heights = jnp.exp(jax.random.uniform(jax.random.fold_in(own, dim), (parts,), jnp.float32, smallest / len(pieces), top_value / len(pieces)))
        loudness = loudness * jnp.repeat(heights, extent[dim] // parts).reshape([-1 if axis == dim else 1 for axis in range(len(extent))])
    return loudness


def scatter_about(key, extent, width, bound, shards=(), held_as=jnp.bfloat16):
    values = width * jax.random.normal(key, extent, jnp.float32)
    if shards:
        values = values * levels(key, extent, shards, -0.22, 0.18)
    return jnp.clip(values, -bound, bound).astype(held_as)


def setup_inputs(seed: int = 0) -> dict:
    key_list = jax.random.split(jax.random.key(seed), 6)
    return {
        "activations": draw_activations(jax.random.fold_in(key_list[5], 71), 0),
        "upstream": draw_upstream(jax.random.fold_in(key_list[5], 71), 0),
        "section_norm_gain": jnp.clip(1.0 + 0.18 * jax.random.normal(key_list[2], (RELAY_SECTIONS, MODEL_WIDTH), jnp.float32), 0.1, 1.9),
        "adapter_down_weight": scatter_about(key_list[3], (RELAY_SECTIONS, ADAPTER_RANK, MODEL_WIDTH), MODEL_WIDTH ** -0.5, 0.078125, ((0, 8),)),
        "adapter_up_weight": scatter_about(key_list[4], (RELAY_SECTIONS, ADAPTER_RANK, MODEL_WIDTH), MODEL_WIDTH ** -0.5, 0.078125, ((0, 8),)),
    }


norm_eps = 1e-05
pair_eps = 1e-06
adapter_scale = 2.0

def replica_backward(inputs, incoming_gradient, gain_row, down_rows, upward_rows):
    widened = inputs.astype(jnp.float32)
    inverse = lax.rsqrt(lax.optimization_barrier(jnp.mean(widened * widened, axis=-1, keepdims=True)) + norm_eps)
    scaled = widened * inverse
    normed = (scaled * gain_row).astype(jnp.bfloat16)
    reduced_gradient = jnp.dot(normed, down_rows.T, preferred_element_type=jnp.float32).astype(jnp.bfloat16)
    count_of_rows = TOK_DEV
    upward_term = adapter_scale * jnp.dot(reduced_gradient.T, incoming_gradient, preferred_element_type=jnp.float32) / count_of_rows
    backward_lowrank = (adapter_scale * jnp.dot(incoming_gradient, upward_rows.T, preferred_element_type=jnp.float32)).astype(jnp.bfloat16)
    down_term = jnp.dot(backward_lowrank.T, normed, preferred_element_type=jnp.float32) / count_of_rows
    back_norm = jnp.dot(backward_lowrank, down_rows, preferred_element_type=jnp.float32) * gain_row
    centre = lax.optimization_barrier(jnp.mean(back_norm * scaled, axis=-1, keepdims=True))
    passed = incoming_gradient.astype(jnp.float32) + inverse * (back_norm - scaled * centre)
    return (passed.astype(jnp.bfloat16), jnp.stack([down_term, upward_term]))

def adasum_levels(vectors):
    for level_bit in range(LEVELS):
        grouped = vectors.reshape(REPLICAS // 2 ** (level_bit + 1), 2, 2 ** level_bit, 2, ADAPTER_RANK * MODEL_WIDTH)
        partner = grouped[:, ::-1].reshape(vectors.shape)
        inner_sum = lax.optimization_barrier(jnp.sum(vectors * partner, axis=-1, keepdims=True))
        own_square = lax.optimization_barrier(jnp.sum(vectors * vectors, axis=-1, keepdims=True))
        far_square = lax.optimization_barrier(jnp.sum(partner * partner, axis=-1, keepdims=True))
        keep_coef = 1.0 - inner_sum / (2.0 * (own_square + pair_eps))
        take_coef = 1.0 - inner_sum / (2.0 * (far_square + pair_eps))
        vectors = keep_coef * vectors + take_coef * partner
    return vectors[0]

def single_section(section_args):
    section_acts, section_grads, gain_row, down_rows, upward_rows = section_args
    section_acts = section_acts.reshape(REPLICAS, TOK_DEV, MODEL_WIDTH)
    section_grads = section_grads.reshape(REPLICAS, TOK_DEV, MODEL_WIDTH)
    passed, gradients = jax.vmap(replica_backward, in_axes=(0, 0, None, None, None))(section_acts, section_grads, gain_row, down_rows, upward_rows)
    merged_gradient = adasum_levels(gradients.reshape(REPLICAS, 2, ADAPTER_RANK * MODEL_WIDTH))
    merged_gradient = merged_gradient.reshape(2 * ADAPTER_RANK * MODEL_WIDTH).astype(jnp.bfloat16)
    return (passed.reshape(ROWS, MODEL_WIDTH), merged_gradient)

def reference(activations, upstream, section_norm_gain, adapter_down_weight, adapter_up_weight):
    passed, merged_gradient = lax.map(single_section, (activations, upstream, section_norm_gain, adapter_down_weight, adapter_up_weight))
    shifted = jnp.concatenate([passed[1:], jnp.zeros_like(passed[:1])], axis=0)
    return (shifted, merged_gradient)
```

```python
import jax
import jax.numpy as jnp
from jax import lax
from jax.sharding import PartitionSpec as P

norm_eps = 1e-05
pair_eps = 1e-06
adapter_scale = 2.0
HIGH = lax.Precision.HIGHEST


def from_behind(x, axis, by):
    size = lax.axis_size(axis)
    pairs = [(i, i + by) for i in range(size) if 0 <= i + by < size]
    return lax.ppermute(x, axis, pairs)


def replica_backward(inputs, incoming_gradient, gain_row, down_rows, upward_rows):
    widened = inputs.astype(jnp.float32)
    inverse = lax.rsqrt(jnp.mean(widened * widened, axis=-1, keepdims=True) + norm_eps)
    scaled = widened * inverse
    normed = (scaled * gain_row).astype(jnp.bfloat16)
    reduced_gradient = jnp.einsum(
        "sh,gh->sg", normed, down_rows, preferred_element_type=jnp.float32
    ).astype(jnp.bfloat16)
    count_of_rows = inputs.shape[0]
    upward_term = (
        adapter_scale
        * jnp.einsum(
            "tk,td->kd", reduced_gradient, incoming_gradient, preferred_element_type=jnp.float32
        )
        / count_of_rows
    )
    backward_lowrank = (
        adapter_scale
        * jnp.einsum(
            "sh,gh->sg", incoming_gradient, upward_rows, preferred_element_type=jnp.float32
        )
    ).astype(jnp.bfloat16)
    down_term = (
        jnp.einsum("tk,td->kd", backward_lowrank, normed, preferred_element_type=jnp.float32)
        / count_of_rows
    )
    back_norm = (
        jnp.einsum("tk,kd->td", backward_lowrank, down_rows, preferred_element_type=jnp.float32)
        * gain_row
    )
    centre = jnp.mean(back_norm * scaled, axis=-1, keepdims=True)
    passed = incoming_gradient.astype(jnp.float32) + inverse * (back_norm - scaled * centre)
    return (passed.astype(jnp.bfloat16), jnp.stack([down_term, upward_term]))


def swap_rows(c, level_bit):
    t, n = c.shape[0], c.shape[1]
    rest = c.shape[2:]
    g = c.reshape((t, n // 2 ** (level_bit + 1), 2, 2 ** level_bit) + rest)
    return g[:, :, ::-1].reshape(c.shape)


def coefficient_tree(gram):
    tensors, n = gram.shape[0], gram.shape[1]
    coef = jnp.broadcast_to(jnp.eye(n, dtype=jnp.float32), (tensors, n, n))
    for level_bit in range(n.bit_length() - 1):
        partner = swap_rows(coef, level_bit)
        gc = jnp.einsum("tra,tab->trb", coef, gram, precision=HIGH)
        inner_sum = jnp.sum(gc * partner, axis=-1, keepdims=True)
        own_square = jnp.sum(gc * coef, axis=-1, keepdims=True)
        far_square = swap_rows(own_square, level_bit)
        keep_coef = 1.0 - inner_sum / (2.0 * (own_square + pair_eps))
        take_coef = 1.0 - inner_sum / (2.0 * (far_square + pair_eps))
        coef = keep_coef * coef + take_coef * partner
    return coef[:, 0, :]


def gram_adasum(grad_pair):
    devices = lax.axis_size("dp")
    me = lax.axis_index("dp")
    flat = grad_pair.reshape(devices, -1)
    chunks = lax.all_to_all(flat, "dp", 0, 0, tiled=True)
    tensors = grad_pair.shape[0]
    per_tensor = devices // tensors
    mine = me // per_tensor
    partial = jnp.dot(chunks, chunks.T, precision=HIGH, preferred_element_type=jnp.float32)
    slot = (jnp.arange(tensors) == mine)[:, None, None]
    gram = lax.psum(jnp.where(slot, partial[None], 0.0), "dp")
    coef = coefficient_tree(gram)
    own_coef = jnp.sum(jnp.where((jnp.arange(tensors) == mine)[:, None], coef, 0.0), axis=0)
    combined = jnp.sum(own_coef[:, None] * chunks, axis=0)
    return combined.astype(jnp.bfloat16)[None]


def per_device(activations, upstream, section_norm_gain, adapter_down_weight, adapter_up_weight):
    passed_local, grad_pair = replica_backward(
        activations[0],
        upstream[0],
        section_norm_gain[0],
        adapter_down_weight[0],
        adapter_up_weight[0],
    )
    shifted = from_behind(passed_local[None], "section", -1)
    merged_gradient = gram_adasum(grad_pair)
    return (shifted, merged_gradient)


def solution(mesh):
    return jax.shard_map(
        per_device,
        mesh=mesh,
        in_specs=(
            P("section", "dp", None),
            P("section", "dp", None),
            P("section", None),
            P("section", None, None),
            P("section", None, None),
        ),
        out_specs=(P("section", "dp", None), P("section", "dp")),
        check_vma=False,
    )
```

```python
import jax
import jax.numpy as jnp
from jax import lax
from jax.sharding import PartitionSpec as P

norm_eps = 1e-05
pair_eps = 1e-06
adapter_scale = 2.0
HIGH = lax.Precision.HIGHEST


def from_behind(x, axis, by):
    size = lax.axis_size(axis)
    pairs = [(i, i + by) for i in range(size) if 0 <= i + by < size]
    return lax.ppermute(x, axis, pairs)


def replica_backward(inputs, incoming_gradient, gain_row, down_rows, upward_rows):
    widened = inputs.astype(jnp.float32)
    inverse = lax.rsqrt(jnp.mean(widened * widened, axis=-1, keepdims=True) + norm_eps)
    scaled = widened * inverse
    normed = (scaled * gain_row).astype(jnp.bfloat16)
    reduced_gradient = jnp.einsum(
        "sh,gh->sg", normed, down_rows, preferred_element_type=jnp.float32
    ).astype(jnp.bfloat16)
    count_of_rows = inputs.shape[0]
    upward_term = (
        adapter_scale
        * jnp.einsum(
            "tk,td->kd", reduced_gradient, incoming_gradient, preferred_element_type=jnp.float32
        )
        / count_of_rows
    )
    backward_lowrank = (
        adapter_scale
        * jnp.einsum(
            "sh,gh->sg", incoming_gradient, upward_rows, preferred_element_type=jnp.float32
        )
    ).astype(jnp.bfloat16)
    down_term = (
        jnp.einsum("tk,td->kd", backward_lowrank, normed, preferred_element_type=jnp.float32)
        / count_of_rows
    )
    back_norm = (
        jnp.einsum("tk,kd->td", backward_lowrank, down_rows, preferred_element_type=jnp.float32)
        * gain_row
    )
    centre = jnp.mean(back_norm * scaled, axis=-1, keepdims=True)
    passed = incoming_gradient.astype(jnp.float32) + inverse * (back_norm - scaled * centre)
    return (passed.astype(jnp.bfloat16), jnp.stack([down_term, upward_term]))


def swap_rows(c, level_bit):
    t, n = c.shape[0], c.shape[1]
    rest = c.shape[2:]
    g = c.reshape((t, n // 2 ** (level_bit + 1), 2, 2 ** level_bit) + rest)
    return g[:, :, ::-1].reshape(c.shape)


def coefficient_tree(gram):
    tensors, n = gram.shape[0], gram.shape[1]
    coef = jnp.broadcast_to(jnp.eye(n, dtype=jnp.float32), (tensors, n, n))
    for level_bit in range(n.bit_length() - 1):
        partner = swap_rows(coef, level_bit)
        gc = jnp.einsum("tra,tab->trb", coef, gram, precision=HIGH)
        inner_sum = jnp.sum(gc * partner, axis=-1, keepdims=True)
        own_square = jnp.sum(gc * coef, axis=-1, keepdims=True)
        far_square = swap_rows(own_square, level_bit)
        keep_coef = 1.0 - inner_sum / (2.0 * (own_square + pair_eps))
        take_coef = 1.0 - inner_sum / (2.0 * (far_square + pair_eps))
        coef = keep_coef * coef + take_coef * partner
    return coef[:, 0, :]


def gram_adasum(grad_pair):
    devices = lax.axis_size("dp")
    me = lax.axis_index("dp")
    flat = grad_pair.reshape(devices, -1)
    chunks = lax.all_to_all(flat, "dp", 0, 0, tiled=True)
    tensors = grad_pair.shape[0]
    per_tensor = devices // tensors
    mine = me // per_tensor
    partial = jnp.dot(chunks, chunks.T, precision=HIGH, preferred_element_type=jnp.float32)
    partials = lax.all_gather(partial, "dp", axis=0, tiled=False)
    gram = jnp.sum(partials.reshape((tensors, per_tensor) + partial.shape), axis=1)
    coef = coefficient_tree(gram)
    own_coef = jnp.sum(jnp.where((jnp.arange(tensors) == mine)[:, None], coef, 0.0), axis=0)
    combined = jnp.sum(own_coef[:, None] * chunks, axis=0)
    return combined.astype(jnp.bfloat16)[None]


def per_device(activations, upstream, section_norm_gain, adapter_down_weight, adapter_up_weight):
    passed_local, grad_pair = replica_backward(
        activations[0],
        upstream[0],
        section_norm_gain[0],
        adapter_down_weight[0],
        adapter_up_weight[0],
    )
    shifted = from_behind(passed_local[None], "section", -1)
    merged_gradient = gram_adasum(grad_pair)
    return (shifted, merged_gradient)


def solution(mesh):
    return jax.shard_map(
        per_device,
        mesh=mesh,
        in_specs=(
            P("section", "dp", None),
            P("section", "dp", None),
            P("section", None),
            P("section", None, None),
            P("section", None, None),
        ),
        out_specs=(P("section", "dp", None), P("section", "dp")),
        check_vma=False,
    )
```

```python
import jax
import jax.numpy as jnp
from jax import lax
from jax.sharding import PartitionSpec as P

norm_eps = 1e-05
pair_eps = 1e-06
adapter_scale = 2.0
HIGH = lax.Precision.HIGHEST


def swapped(value, axis, bit):
    mask = 2**bit
    pairs = [(source, source ^ mask) for source in range(lax.axis_size(axis))]
    return lax.ppermute(value, axis, pairs)


def from_behind(x, axis, by):
    size = lax.axis_size(axis)
    pairs = [(i, i + by) for i in range(size) if 0 <= i + by < size]
    return lax.ppermute(x, axis, pairs)


def replica_backward(inputs, incoming_gradient, gain_row, down_rows, upward_rows):
    widened = inputs.astype(jnp.float32)
    inverse = lax.rsqrt(jnp.mean(widened * widened, axis=-1, keepdims=True) + norm_eps)
    scaled = widened * inverse
    normed = (scaled * gain_row).astype(jnp.bfloat16)
    reduced_gradient = jnp.einsum(
        "sh,gh->sg", normed, down_rows, preferred_element_type=jnp.float32
    ).astype(jnp.bfloat16)
    count_of_rows = inputs.shape[0]
    upward_term = (
        adapter_scale
        * jnp.einsum(
            "tk,td->kd", reduced_gradient, incoming_gradient, preferred_element_type=jnp.float32
        )
        / count_of_rows
    )
    backward_lowrank = (
        adapter_scale
        * jnp.einsum(
            "sh,gh->sg", incoming_gradient, upward_rows, preferred_element_type=jnp.float32
        )
    ).astype(jnp.bfloat16)
    down_term = (
        jnp.einsum("tk,td->kd", backward_lowrank, normed, preferred_element_type=jnp.float32)
        / count_of_rows
    )
    back_norm = (
        jnp.einsum("tk,kd->td", backward_lowrank, down_rows, preferred_element_type=jnp.float32)
        * gain_row
    )
    centre = jnp.mean(back_norm * scaled, axis=-1, keepdims=True)
    passed = incoming_gradient.astype(jnp.float32) + inverse * (back_norm - scaled * centre)
    return (passed.astype(jnp.bfloat16), jnp.stack([down_term, upward_term]))


def swap_rows(c, level_bit):
    t, n = c.shape[0], c.shape[1]
    rest = c.shape[2:]
    g = c.reshape((t, n // 2 ** (level_bit + 1), 2, 2 ** level_bit) + rest)
    return g[:, :, ::-1].reshape(c.shape)


def coefficient_tree(gram):
    tensors, n = gram.shape[0], gram.shape[1]
    coef = jnp.broadcast_to(jnp.eye(n, dtype=jnp.float32), (tensors, n, n))
    for level_bit in range(n.bit_length() - 1):
        partner = swap_rows(coef, level_bit)
        gc = jnp.einsum("tra,tab->trb", coef, gram, precision=HIGH)
        inner_sum = jnp.sum(gc * partner, axis=-1, keepdims=True)
        own_square = jnp.sum(gc * coef, axis=-1, keepdims=True)
        far_square = swap_rows(own_square, level_bit)
        keep_coef = 1.0 - inner_sum / (2.0 * (own_square + pair_eps))
        take_coef = 1.0 - inner_sum / (2.0 * (far_square + pair_eps))
        coef = keep_coef * coef + take_coef * partner
    return coef[:, 0, :]


def gram_adasum(grad_pair):
    devices = lax.axis_size("dp")
    me = lax.axis_index("dp")
    flat = grad_pair.reshape(devices, -1)
    chunks = lax.all_to_all(flat, "dp", 0, 0, tiled=True)
    tensors = grad_pair.shape[0]
    per_tensor = devices // tensors
    mine = me // per_tensor
    partial = jnp.dot(chunks, chunks.T, precision=HIGH, preferred_element_type=jnp.float32)
    half_bits = per_tensor.bit_length() - 1
    for level_bit in range(half_bits):
        partial = partial + swapped(partial, "dp", level_bit)
    other = swapped(partial, "dp", half_bits)
    gram = jnp.where(mine == 0, jnp.stack([partial, other]), jnp.stack([other, partial]))
    coef = coefficient_tree(gram)
    own_coef = jnp.sum(jnp.where((jnp.arange(tensors) == mine)[:, None], coef, 0.0), axis=0)
    combined = jnp.sum(own_coef[:, None] * chunks, axis=0)
    return combined.astype(jnp.bfloat16)[None]


def per_device(activations, upstream, section_norm_gain, adapter_down_weight, adapter_up_weight):
    passed_local, grad_pair = replica_backward(
        activations[0],
        upstream[0],
        section_norm_gain[0],
        adapter_down_weight[0],
        adapter_up_weight[0],
    )
    shifted = from_behind(passed_local[None], "section", -1)
    merged_gradient = gram_adasum(grad_pair)
    return (shifted, merged_gradient)


def solution(mesh):
    return jax.shard_map(
        per_device,
        mesh=mesh,
        in_specs=(
            P("section", "dp", None),
            P("section", "dp", None),
            P("section", None),
            P("section", None, None),
            P("section", None, None),
        ),
        out_specs=(P("section", "dp", None), P("section", "dp")),
        check_vma=False,
    )
```

```python
import jax
import jax.numpy as jnp
from jax import lax
from jax.sharding import PartitionSpec as P

norm_eps = 1e-05
pair_eps = 1e-06
adapter_scale = 2.0
HIGH = lax.Precision.HIGHEST


def swapped(value, axis, bit):
    mask = 2**bit
    pairs = [(source, source ^ mask) for source in range(lax.axis_size(axis))]
    return lax.ppermute(value, axis, pairs)


def swapped_by(value, axis, mask):
    pairs = [(source, source ^ mask) for source in range(lax.axis_size(axis))]
    return lax.ppermute(value, axis, pairs)


def from_behind(x, axis, by):
    size = lax.axis_size(axis)
    pairs = [(i, i + by) for i in range(size) if 0 <= i + by < size]
    return lax.ppermute(x, axis, pairs)


def replica_backward(inputs, incoming_gradient, gain_row, down_rows, upward_rows):
    widened = inputs.astype(jnp.float32)
    inverse = lax.rsqrt(jnp.mean(widened * widened, axis=-1, keepdims=True) + norm_eps)
    scaled = widened * inverse
    normed = (scaled * gain_row).astype(jnp.bfloat16)
    reduced_gradient = jnp.einsum(
        "sh,gh->sg", normed, down_rows, preferred_element_type=jnp.float32
    ).astype(jnp.bfloat16)
    count_of_rows = inputs.shape[0]
    upward_term = (
        adapter_scale
        * jnp.einsum(
            "tk,td->kd", reduced_gradient, incoming_gradient, preferred_element_type=jnp.float32
        )
        / count_of_rows
    )
    backward_lowrank = (
        adapter_scale
        * jnp.einsum(
            "sh,gh->sg", incoming_gradient, upward_rows, preferred_element_type=jnp.float32
        )
    ).astype(jnp.bfloat16)
    down_term = (
        jnp.einsum("tk,td->kd", backward_lowrank, normed, preferred_element_type=jnp.float32)
        / count_of_rows
    )
    back_norm = (
        jnp.einsum("tk,kd->td", backward_lowrank, down_rows, preferred_element_type=jnp.float32)
        * gain_row
    )
    centre = jnp.mean(back_norm * scaled, axis=-1, keepdims=True)
    passed = incoming_gradient.astype(jnp.float32) + inverse * (back_norm - scaled * centre)
    return (passed.astype(jnp.bfloat16), jnp.stack([down_term, upward_term]))


def coefficient_tree(gram):
    tensors, n = gram.shape[0], gram.shape[1]
    h = gram
    coef = jnp.ones((tensors, n), jnp.float32)
    for level_bit in range(n.bit_length() - 1):
        m = h.shape[1] // 2
        h4 = h.reshape(tensors, m, 2, m, 2)
        diag = jnp.diagonal(h, axis1=1, axis2=2).reshape(tensors, m, 2)
        own_square, far_square = diag[..., 0], diag[..., 1]
        inner_sum = jnp.diagonal(h4[:, :, 0, :, 1], axis1=1, axis2=2)
        keep_coef = 1.0 - inner_sum / (2.0 * (own_square + pair_eps))
        take_coef = 1.0 - inner_sum / (2.0 * (far_square + pair_eps))
        weights = jnp.stack([keep_coef, take_coef], axis=-1)
        h = jnp.sum(
            weights[:, :, :, None, None] * h4 * weights[:, None, None, :, :], axis=(2, 4)
        )
        coef = (coef.reshape(tensors, m, 2, 2**level_bit) * weights[..., None]).reshape(tensors, n)
    return coef


def gram_adasum(grad_pair):
    devices = lax.axis_size("dp")
    me = lax.axis_index("dp")
    flat = grad_pair.reshape(devices, -1)
    chunks = lax.all_to_all(flat, "dp", 0, 0, tiled=True)
    tensors = grad_pair.shape[0]
    per_tensor = devices // tensors
    mine = me // per_tensor
    partial = jnp.dot(chunks, chunks.T, precision=HIGH, preferred_element_type=jnp.float32)
    for low in (0, 2):
        one, two, three = (swapped_by(partial, "dp", mask << low) for mask in (1, 2, 3))
        partial = (partial + one) + (two + three)
    same, other_a, other_b = (swapped_by(partial, "dp", mask << 4) for mask in (1, 2, 3))
    partial = partial + same
    other = other_a + other_b
    gram = jnp.where(mine == 0, jnp.stack([partial, other]), jnp.stack([other, partial]))
    coef = coefficient_tree(gram)
    own_coef = jnp.sum(jnp.where((jnp.arange(tensors) == mine)[:, None], coef, 0.0), axis=0)
    combined = jnp.sum(own_coef[:, None] * chunks, axis=0)
    return combined.astype(jnp.bfloat16)[None]


def per_device(activations, upstream, section_norm_gain, adapter_down_weight, adapter_up_weight):
    passed_local, grad_pair = replica_backward(
        activations[0],
        upstream[0],
        section_norm_gain[0],
        adapter_down_weight[0],
        adapter_up_weight[0],
    )
    shifted = from_behind(passed_local[None], "section", -1)
    merged_gradient = gram_adasum(grad_pair)
    return (shifted, merged_gradient)


def solution(mesh):
    return jax.shard_map(
        per_device,
        mesh=mesh,
        in_specs=(
            P("section", "dp", None),
            P("section", "dp", None),
            P("section", None),
            P("section", None, None),
            P("section", None, None),
        ),
        out_specs=(P("section", "dp", None), P("section", "dp")),
        check_vma=False,
    )
```

```python
import jax
import jax.numpy as jnp
from jax import lax
from jax.sharding import PartitionSpec as P

norm_eps = 1e-05
pair_eps = 1e-06
adapter_scale = 2.0
HIGH = lax.Precision.HIGHEST


def swapped(value, axis, bit):
    mask = 2**bit
    pairs = [(source, source ^ mask) for source in range(lax.axis_size(axis))]
    return lax.ppermute(value, axis, pairs)


def from_behind(x, axis, by):
    size = lax.axis_size(axis)
    pairs = [(i, i + by) for i in range(size) if 0 <= i + by < size]
    return lax.ppermute(x, axis, pairs)


def replica_backward(inputs, incoming_gradient, gain_row, down_rows, upward_rows):
    widened = inputs.astype(jnp.float32)
    inverse = lax.rsqrt(jnp.mean(widened * widened, axis=-1, keepdims=True) + norm_eps)
    scaled = widened * inverse
    normed = (scaled * gain_row).astype(jnp.bfloat16)
    reduced_gradient = jnp.einsum(
        "sh,gh->sg", normed, down_rows, preferred_element_type=jnp.float32
    ).astype(jnp.bfloat16)
    count_of_rows = inputs.shape[0]
    upward_term = (
        adapter_scale
        * jnp.einsum(
            "tk,td->kd", reduced_gradient, incoming_gradient, preferred_element_type=jnp.float32
        )
        / count_of_rows
    )
    backward_lowrank = (
        adapter_scale
        * jnp.einsum(
            "sh,gh->sg", incoming_gradient, upward_rows, preferred_element_type=jnp.float32
        )
    ).astype(jnp.bfloat16)
    down_term = (
        jnp.einsum("tk,td->kd", backward_lowrank, normed, preferred_element_type=jnp.float32)
        / count_of_rows
    )
    back_norm = (
        jnp.einsum("tk,kd->td", backward_lowrank, down_rows, preferred_element_type=jnp.float32)
        * gain_row
    )
    centre = jnp.mean(back_norm * scaled, axis=-1, keepdims=True)
    passed = incoming_gradient.astype(jnp.float32) + inverse * (back_norm - scaled * centre)
    return (passed.astype(jnp.bfloat16), jnp.stack([down_term, upward_term]))


def swap_rows(c, level_bit):
    t, n = c.shape[0], c.shape[1]
    rest = c.shape[2:]
    g = c.reshape((t, n // 2 ** (level_bit + 1), 2, 2 ** level_bit) + rest)
    return g[:, :, ::-1].reshape(c.shape)


def coefficient_tree(gram):
    tensors, n = gram.shape[0], gram.shape[1]
    coef = jnp.broadcast_to(jnp.eye(n, dtype=jnp.float32), (tensors, n, n))
    for level_bit in range(n.bit_length() - 1):
        partner = swap_rows(coef, level_bit)
        gc = jnp.einsum("tra,tab->trb", coef, gram, precision=HIGH)
        inner_sum = jnp.sum(gc * partner, axis=-1, keepdims=True)
        own_square = jnp.sum(gc * coef, axis=-1, keepdims=True)
        far_square = swap_rows(own_square, level_bit)
        keep_coef = 1.0 - inner_sum / (2.0 * (own_square + pair_eps))
        take_coef = 1.0 - inner_sum / (2.0 * (far_square + pair_eps))
        coef = keep_coef * coef + take_coef * partner
    return coef[:, 0, :]


def gram_adasum(grad_pair):
    devices = lax.axis_size("dp")
    me = lax.axis_index("dp")
    flat = grad_pair.reshape(devices, -1)
    chunks = lax.all_to_all(flat, "dp", 0, 0, tiled=True)
    tensors = grad_pair.shape[0]
    per_tensor = devices // tensors
    mine = me // per_tensor
    partial = jnp.dot(chunks, chunks.T, precision=HIGH, preferred_element_type=jnp.float32)
    rows = lax.all_to_all(partial[:, None, :], "dp", 0, 0, tiled=True)
    rows = jnp.sum(rows.reshape(tensors, per_tensor, partial.shape[1]), axis=1)
    spread = jnp.broadcast_to(rows[None], (devices, tensors, partial.shape[1]))
    gathered = lax.all_to_all(spread, "dp", 0, 0, tiled=True)
    gram = jnp.swapaxes(gathered, 0, 1)
    coef = coefficient_tree(gram)
    own_coef = jnp.sum(jnp.where((jnp.arange(tensors) == mine)[:, None], coef, 0.0), axis=0)
    combined = jnp.sum(own_coef[:, None] * chunks, axis=0)
    return combined.astype(jnp.bfloat16)[None]


def per_device(activations, upstream, section_norm_gain, adapter_down_weight, adapter_up_weight):
    passed_local, grad_pair = replica_backward(
        activations[0],
        upstream[0],
        section_norm_gain[0],
        adapter_down_weight[0],
        adapter_up_weight[0],
    )
    shifted = from_behind(passed_local[None], "section", -1)
    merged_gradient = gram_adasum(grad_pair)
    return (shifted, merged_gradient)


def solution(mesh):
    return jax.shard_map(
        per_device,
        mesh=mesh,
        in_specs=(
            P("section", "dp", None),
            P("section", "dp", None),
            P("section", None),
            P("section", None, None),
            P("section", None, None),
        ),
        out_specs=(P("section", "dp", None), P("section", "dp")),
        check_vma=False,
    )
```

```python
import jax
import jax.numpy as jnp
from jax import lax
from jax.sharding import PartitionSpec as P
from jax.experimental import pallas as pl

norm_eps = 1e-05
pair_eps = 1e-06
adapter_scale = 2.0
HIGH = lax.Precision.HIGHEST


def swapped(value, axis, bit):
    mask = 2**bit
    pairs = [(source, source ^ mask) for source in range(lax.axis_size(axis))]
    return lax.ppermute(value, axis, pairs)


def from_behind(x, axis, by):
    size = lax.axis_size(axis)
    pairs = [(i, i + by) for i in range(size) if 0 <= i + by < size]
    return lax.ppermute(x, axis, pairs)


def replica_backward(inputs, incoming_gradient, gain_row, down_rows, upward_rows):
    widened = inputs.astype(jnp.float32)
    inverse = lax.rsqrt(jnp.mean(widened * widened, axis=-1, keepdims=True) + norm_eps)
    scaled = widened * inverse
    normed = (scaled * gain_row).astype(jnp.bfloat16)
    reduced_gradient = jnp.einsum(
        "sh,gh->sg", normed, down_rows, preferred_element_type=jnp.float32
    ).astype(jnp.bfloat16)
    count_of_rows = inputs.shape[0]
    upward_term = (
        adapter_scale
        * jnp.einsum(
            "tk,td->kd", reduced_gradient, incoming_gradient, preferred_element_type=jnp.float32
        )
        / count_of_rows
    )
    backward_lowrank = (
        adapter_scale
        * jnp.einsum(
            "sh,gh->sg", incoming_gradient, upward_rows, preferred_element_type=jnp.float32
        )
    ).astype(jnp.bfloat16)
    down_term = (
        jnp.einsum("tk,td->kd", backward_lowrank, normed, preferred_element_type=jnp.float32)
        / count_of_rows
    )
    back_norm = (
        jnp.einsum("tk,kd->td", backward_lowrank, down_rows, preferred_element_type=jnp.float32)
        * gain_row
    )
    centre = jnp.mean(back_norm * scaled, axis=-1, keepdims=True)
    passed = incoming_gradient.astype(jnp.float32) + inverse * (back_norm - scaled * centre)
    return (passed.astype(jnp.bfloat16), jnp.stack([down_term, upward_term]))


def swap_rows(c, level_bit):
    t, n = c.shape[0], c.shape[1]
    rest = c.shape[2:]
    g = c.reshape((t, n // 2 ** (level_bit + 1), 2, 2 ** level_bit) + rest)
    return g[:, :, ::-1].reshape(c.shape)


def coefficient_tree(gram):
    tensors, n = gram.shape[0], gram.shape[1]
    coef = jnp.broadcast_to(jnp.eye(n, dtype=jnp.float32), (tensors, n, n))
    for level_bit in range(n.bit_length() - 1):
        partner = swap_rows(coef, level_bit)
        gc = jnp.einsum("tra,tab->trb", coef, gram, precision=HIGH)
        inner_sum = jnp.sum(gc * partner, axis=-1, keepdims=True)
        own_square = jnp.sum(gc * coef, axis=-1, keepdims=True)
        far_square = swap_rows(own_square, level_bit)
        keep_coef = 1.0 - inner_sum / (2.0 * (own_square + pair_eps))
        take_coef = 1.0 - inner_sum / (2.0 * (far_square + pair_eps))
        coef = keep_coef * coef + take_coef * partner
    return coef[:, 0, :]


def tree_kernel(gram_ref, out_ref):
    n = gram_ref.shape[1]
    rows = lax.broadcasted_iota(jnp.int32, (n, n), 0)
    cols = lax.broadcasted_iota(jnp.int32, (n, n), 1)
    eye = (rows == cols).astype(jnp.float32)
    for t in range(gram_ref.shape[0]):
        gram = gram_ref[t]
        coef = eye
        for level_bit in range(n.bit_length() - 1):
            swap = (cols == jnp.bitwise_xor(rows, 2**level_bit)).astype(jnp.float32)
            partner = jnp.dot(swap, coef, precision=HIGH, preferred_element_type=jnp.float32)
            gc = jnp.dot(coef, gram, precision=HIGH, preferred_element_type=jnp.float32)
            gp = jnp.dot(partner, gram, precision=HIGH, preferred_element_type=jnp.float32)
            inner_sum = jnp.sum(gc * partner, axis=1, keepdims=True)
            own_square = jnp.sum(gc * coef, axis=1, keepdims=True)
            far_square = jnp.sum(gp * partner, axis=1, keepdims=True)
            keep_coef = 1.0 - inner_sum / (2.0 * (own_square + pair_eps))
            take_coef = 1.0 - inner_sum / (2.0 * (far_square + pair_eps))
            coef = keep_coef * coef + take_coef * partner
        out_ref[t] = coef[0:8, :]


def tree_coefficients(gram, interpret=False):
    tensors, n = gram.shape[0], gram.shape[1]
    rows = pl.pallas_call(
        tree_kernel,
        out_shape=jax.ShapeDtypeStruct((tensors, 8, n), jnp.float32),
        interpret=interpret,
    )(gram)
    return rows[:, 0, :]


def gram_adasum(grad_pair):
    devices = lax.axis_size("dp")
    me = lax.axis_index("dp")
    flat = grad_pair.reshape(devices, -1)
    chunks = lax.all_to_all(flat, "dp", 0, 0, tiled=True)
    tensors = grad_pair.shape[0]
    per_tensor = devices // tensors
    mine = me // per_tensor
    partial = jnp.dot(chunks, chunks.T, precision=HIGH, preferred_element_type=jnp.float32)
    rows = lax.all_to_all(partial[:, None, :], "dp", 0, 0, tiled=True)
    rows = jnp.sum(rows.reshape(tensors, per_tensor, partial.shape[1]), axis=1)
    spread = jnp.broadcast_to(rows[None], (devices, tensors, partial.shape[1]))
    gathered = lax.all_to_all(spread, "dp", 0, 0, tiled=True)
    gram = jnp.swapaxes(gathered, 0, 1)
    coef = tree_coefficients(gram)
    own_coef = jnp.sum(jnp.where((jnp.arange(tensors) == mine)[:, None], coef, 0.0), axis=0)
    combined = jnp.sum(own_coef[:, None] * chunks, axis=0)
    return combined.astype(jnp.bfloat16)[None]


def per_device(activations, upstream, section_norm_gain, adapter_down_weight, adapter_up_weight):
    passed_local, grad_pair = replica_backward(
        activations[0],
        upstream[0],
        section_norm_gain[0],
        adapter_down_weight[0],
        adapter_up_weight[0],
    )
    shifted = from_behind(passed_local[None], "section", -1)
    merged_gradient = gram_adasum(grad_pair)
    return (shifted, merged_gradient)


def solution(mesh):
    return jax.shard_map(
        per_device,
        mesh=mesh,
        in_specs=(
            P("section", "dp", None),
            P("section", "dp", None),
            P("section", None),
            P("section", None, None),
            P("section", None, None),
        ),
        out_specs=(P("section", "dp", None), P("section", "dp")),
        check_vma=False,
    )
```

```python
import numpy as np
import jax
import jax.numpy as jnp
from jax import lax
from jax.sharding import PartitionSpec as P
from jax.experimental import pallas as pl

norm_eps = 1e-05
pair_eps = 1e-06
adapter_scale = 2.0
HIGH = lax.Precision.HIGHEST


def swapped(value, axis, bit):
    mask = 2**bit
    pairs = [(source, source ^ mask) for source in range(lax.axis_size(axis))]
    return lax.ppermute(value, axis, pairs)


def from_behind(x, axis, by):
    size = lax.axis_size(axis)
    pairs = [(i, i + by) for i in range(size) if 0 <= i + by < size]
    return lax.ppermute(x, axis, pairs)


def replica_backward(inputs, incoming_gradient, gain_row, down_rows, upward_rows):
    widened = inputs.astype(jnp.float32)
    inverse = lax.rsqrt(jnp.mean(widened * widened, axis=-1, keepdims=True) + norm_eps)
    scaled = widened * inverse
    normed = (scaled * gain_row).astype(jnp.bfloat16)
    reduced_gradient = jnp.einsum(
        "sh,gh->sg", normed, down_rows, preferred_element_type=jnp.float32
    ).astype(jnp.bfloat16)
    count_of_rows = inputs.shape[0]
    upward_term = (
        adapter_scale
        * jnp.einsum(
            "tk,td->kd", reduced_gradient, incoming_gradient, preferred_element_type=jnp.float32
        )
        / count_of_rows
    )
    backward_lowrank = (
        adapter_scale
        * jnp.einsum(
            "sh,gh->sg", incoming_gradient, upward_rows, preferred_element_type=jnp.float32
        )
    ).astype(jnp.bfloat16)
    down_term = (
        jnp.einsum("tk,td->kd", backward_lowrank, normed, preferred_element_type=jnp.float32)
        / count_of_rows
    )
    back_norm = (
        jnp.einsum("tk,kd->td", backward_lowrank, down_rows, preferred_element_type=jnp.float32)
        * gain_row
    )
    centre = jnp.mean(back_norm * scaled, axis=-1, keepdims=True)
    passed = incoming_gradient.astype(jnp.float32) + inverse * (back_norm - scaled * centre)
    return (passed.astype(jnp.bfloat16), jnp.stack([down_term, upward_term]))


def swap_rows(c, level_bit):
    t, n = c.shape[0], c.shape[1]
    rest = c.shape[2:]
    g = c.reshape((t, n // 2 ** (level_bit + 1), 2, 2 ** level_bit) + rest)
    return g[:, :, ::-1].reshape(c.shape)


def coefficient_tree(gram):
    tensors, n = gram.shape[0], gram.shape[1]
    coef = jnp.broadcast_to(jnp.eye(n, dtype=jnp.float32), (tensors, n, n))
    for level_bit in range(n.bit_length() - 1):
        partner = swap_rows(coef, level_bit)
        gc = jnp.einsum("tra,tab->trb", coef, gram, precision=HIGH)
        inner_sum = jnp.sum(gc * partner, axis=-1, keepdims=True)
        own_square = jnp.sum(gc * coef, axis=-1, keepdims=True)
        far_square = swap_rows(own_square, level_bit)
        keep_coef = 1.0 - inner_sum / (2.0 * (own_square + pair_eps))
        take_coef = 1.0 - inner_sum / (2.0 * (far_square + pair_eps))
        coef = keep_coef * coef + take_coef * partner
    return coef[:, 0, :]


def bit_reversed_eye(n):
    bits = n.bit_length() - 1
    order = [int(format(i, f"0{bits}b")[::-1], 2) for i in range(n)]
    return np.eye(n, dtype=np.float32)[order]


def combine_kernel(start_ref, gram_ref, sel_ref, chunks_ref, out_ref):
    n = gram_ref.shape[0]
    finals = []
    for t in range(gram_ref.shape[1] // n):
        gram = gram_ref[:, t * n:(t + 1) * n]
        coef = start_ref[...]
        while coef.shape[0] > 1:
            half = coef.shape[0] // 2
            first, second = coef[:half], coef[half:]
            g_first = jnp.dot(first, gram, precision=HIGH, preferred_element_type=jnp.float32)
            g_second = jnp.dot(second, gram, precision=HIGH, preferred_element_type=jnp.float32)
            inner_sum = jnp.sum(g_first * second, axis=1, keepdims=True)
            own_square = jnp.sum(g_first * first, axis=1, keepdims=True)
            far_square = jnp.sum(g_second * second, axis=1, keepdims=True)
            keep_coef = 1.0 - inner_sum / (2.0 * (own_square + pair_eps))
            take_coef = 1.0 - inner_sum / (2.0 * (far_square + pair_eps))
            coef = keep_coef * first + take_coef * second
        finals.append(coef)
    sel = sel_ref[0:1, 0:n]
    row = sel * finals[0] + (1.0 - sel) * finals[1]
    eye = start_ref[...] * 0.0 + (
        lax.broadcasted_iota(jnp.int32, (n, n), 0) == lax.broadcasted_iota(jnp.int32, (n, n), 1)
    ).astype(jnp.float32)
    column = lax.dot_general(
        eye, row, (((1,), (1,)), ((), ())), precision=HIGH, preferred_element_type=jnp.float32
    )
    combined = jnp.sum(column * chunks_ref[...], axis=0, keepdims=True)
    out_ref[...] = combined.astype(out_ref.dtype)


def combine(gram_rows, first_tensor, chunks, interpret=False):
    n = gram_rows.shape[0]
    sel = jnp.broadcast_to(first_tensor.astype(jnp.float32), (8, 128))
    return pl.pallas_call(
        combine_kernel,
        out_shape=jax.ShapeDtypeStruct((1, chunks.shape[1]), jnp.bfloat16),
        interpret=interpret,
    )(jnp.asarray(bit_reversed_eye(n)), gram_rows, sel, chunks)


def gram_adasum(grad_pair):
    devices = lax.axis_size("dp")
    me = lax.axis_index("dp")
    flat = grad_pair.reshape(devices, -1)
    chunks = lax.all_to_all(flat, "dp", 0, 0, tiled=True)
    tensors = grad_pair.shape[0]
    per_tensor = devices // tensors
    mine = me // per_tensor
    partial = jnp.dot(chunks, chunks.T, precision=HIGH, preferred_element_type=jnp.float32)
    rows = lax.all_to_all(partial[:, None, :], "dp", 0, 0, tiled=True)
    rows = jnp.sum(rows.reshape(tensors, per_tensor, partial.shape[1]), axis=1)
    spread = jnp.broadcast_to(rows.reshape(1, -1), (devices, tensors * partial.shape[1]))
    gram_rows = lax.all_to_all(spread, "dp", 0, 0, tiled=True)
    return combine(gram_rows, mine == 0, chunks)


def per_device(activations, upstream, section_norm_gain, adapter_down_weight, adapter_up_weight):
    passed_local, grad_pair = replica_backward(
        activations[0],
        upstream[0],
        section_norm_gain[0],
        adapter_down_weight[0],
        adapter_up_weight[0],
    )
    shifted = from_behind(passed_local[None], "section", -1)
    merged_gradient = gram_adasum(grad_pair)
    return (shifted, merged_gradient)


def solution(mesh):
    return jax.shard_map(
        per_device,
        mesh=mesh,
        in_specs=(
            P("section", "dp", None),
            P("section", "dp", None),
            P("section", None),
            P("section", None, None),
            P("section", None, None),
        ),
        out_specs=(P("section", "dp", None), P("section", "dp")),
        check_vma=False,
    )
```

```python
import numpy as np
import jax
import jax.numpy as jnp
from jax import lax
from jax.sharding import Mesh, PartitionSpec as P
from jax.experimental import pallas as pl

norm_eps = 1e-05
pair_eps = 1e-06
adapter_scale = 2.0
HIGH = lax.Precision.HIGHEST


def swapped(value, axis, bit):
    mask = 2**bit
    pairs = [(source, source ^ mask) for source in range(lax.axis_size(axis))]
    return lax.ppermute(value, axis, pairs)


def from_behind(x, axis, by):
    size = lax.axis_size(axis)
    pairs = [(i, i + by) for i in range(size) if 0 <= i + by < size]
    return lax.ppermute(x, axis, pairs)


def replica_backward(inputs, incoming_gradient, gain_row, down_rows, upward_rows):
    widened = inputs.astype(jnp.float32)
    inverse = lax.rsqrt(jnp.mean(widened * widened, axis=-1, keepdims=True) + norm_eps)
    scaled = widened * inverse
    normed = (scaled * gain_row).astype(jnp.bfloat16)
    reduced_gradient = jnp.einsum(
        "sh,gh->sg", normed, down_rows, preferred_element_type=jnp.float32
    ).astype(jnp.bfloat16)
    count_of_rows = inputs.shape[0]
    upward_term = (
        adapter_scale
        * jnp.einsum(
            "tk,td->kd", reduced_gradient, incoming_gradient, preferred_element_type=jnp.float32
        )
        / count_of_rows
    )
    backward_lowrank = (
        adapter_scale
        * jnp.einsum(
            "sh,gh->sg", incoming_gradient, upward_rows, preferred_element_type=jnp.float32
        )
    ).astype(jnp.bfloat16)
    down_term = (
        jnp.einsum("tk,td->kd", backward_lowrank, normed, preferred_element_type=jnp.float32)
        / count_of_rows
    )
    back_norm = (
        jnp.einsum("tk,kd->td", backward_lowrank, down_rows, preferred_element_type=jnp.float32)
        * gain_row
    )
    centre = jnp.mean(back_norm * scaled, axis=-1, keepdims=True)
    passed = incoming_gradient.astype(jnp.float32) + inverse * (back_norm - scaled * centre)
    return (passed.astype(jnp.bfloat16), jnp.stack([down_term, upward_term]))


def swap_rows(c, level_bit):
    t, n = c.shape[0], c.shape[1]
    rest = c.shape[2:]
    g = c.reshape((t, n // 2 ** (level_bit + 1), 2, 2 ** level_bit) + rest)
    return g[:, :, ::-1].reshape(c.shape)


def coefficient_tree(gram):
    tensors, n = gram.shape[0], gram.shape[1]
    coef = jnp.broadcast_to(jnp.eye(n, dtype=jnp.float32), (tensors, n, n))
    for level_bit in range(n.bit_length() - 1):
        partner = swap_rows(coef, level_bit)
        gc = jnp.einsum("tra,tab->trb", coef, gram, precision=HIGH)
        inner_sum = jnp.sum(gc * partner, axis=-1, keepdims=True)
        own_square = jnp.sum(gc * coef, axis=-1, keepdims=True)
        far_square = swap_rows(own_square, level_bit)
        keep_coef = 1.0 - inner_sum / (2.0 * (own_square + pair_eps))
        take_coef = 1.0 - inner_sum / (2.0 * (far_square + pair_eps))
        coef = keep_coef * coef + take_coef * partner
    return coef[:, 0, :]


def bit_reversed_eye(n):
    bits = n.bit_length() - 1
    order = [int(format(i, f"0{bits}b")[::-1], 2) for i in range(n)]
    return np.eye(n, dtype=np.float32)[order]


def combine_kernel(start_ref, gram_ref, sel_ref, chunks_ref, out_ref):
    n = gram_ref.shape[0]
    finals = []
    for t in range(gram_ref.shape[1] // n):
        gram = gram_ref[:, t * n:(t + 1) * n]
        coef = start_ref[...]
        while coef.shape[0] > 1:
            half = coef.shape[0] // 2
            first, second = coef[:half], coef[half:]
            g_first = jnp.dot(first, gram, precision=HIGH, preferred_element_type=jnp.float32)
            g_second = jnp.dot(second, gram, precision=HIGH, preferred_element_type=jnp.float32)
            inner_sum = jnp.sum(g_first * second, axis=1, keepdims=True)
            own_square = jnp.sum(g_first * first, axis=1, keepdims=True)
            far_square = jnp.sum(g_second * second, axis=1, keepdims=True)
            keep_coef = 1.0 - inner_sum / (2.0 * (own_square + pair_eps))
            take_coef = 1.0 - inner_sum / (2.0 * (far_square + pair_eps))
            coef = keep_coef * first + take_coef * second
        finals.append(coef)
    sel = sel_ref[0:1, 0:n]
    row = sel * finals[0] + (1.0 - sel) * finals[1]
    eye = start_ref[...] * 0.0 + (
        lax.broadcasted_iota(jnp.int32, (n, n), 0) == lax.broadcasted_iota(jnp.int32, (n, n), 1)
    ).astype(jnp.float32)
    column = lax.dot_general(
        eye, row, (((1,), (1,)), ((), ())), precision=HIGH, preferred_element_type=jnp.float32
    )
    combined = jnp.sum(column * chunks_ref[...], axis=0, keepdims=True)
    out_ref[...] = combined.astype(out_ref.dtype)


def combine(gram_rows, first_tensor, chunks, interpret=False):
    n = gram_rows.shape[0]
    sel = jnp.broadcast_to(first_tensor.astype(jnp.float32), (8, 128))
    return pl.pallas_call(
        combine_kernel,
        out_shape=jax.ShapeDtypeStruct((1, chunks.shape[1]), jnp.bfloat16),
        interpret=interpret,
    )(jnp.asarray(bit_reversed_eye(n)), gram_rows, sel, chunks)


def gram_adasum(grad_pair):
    ny, nz = lax.axis_size("y"), lax.axis_size("z")
    devices = ny * nz
    me = lax.axis_index("y") * nz + lax.axis_index("z")
    flat = grad_pair.reshape(devices, -1)
    chunks = lax.all_to_all(flat, ("y", "z"), 0, 0, tiled=True)
    tensors = grad_pair.shape[0]
    per_tensor = devices // tensors
    mine = me // per_tensor
    n = devices
    partial = jnp.dot(chunks, chunks.T, precision=HIGH, preferred_element_type=jnp.float32)
    part_z = lax.all_to_all(partial.reshape(nz, ny, n), "z", 0, 0, tiled=True)
    part_z = jnp.sum(part_z.reshape(nz, ny, n), axis=0)
    part_y = lax.all_to_all(part_z, "y", 0, 0, tiled=True)
    rows = jnp.sum(part_y.reshape(tensors, ny // tensors, n), axis=1)
    spread_y = jnp.broadcast_to(rows.reshape(1, tensors * n), (ny, tensors * n))
    got_y = lax.all_to_all(spread_y, "y", 0, 0, tiled=True)
    spread_z = jnp.broadcast_to(got_y.reshape(1, ny * tensors * n), (nz, ny * tensors * n))
    got_z = lax.all_to_all(spread_z, "z", 0, 0, tiled=True)
    gram_rows = got_z.reshape(n, tensors * n)
    return combine(gram_rows, mine == 0, chunks)


def per_device(activations, upstream, section_norm_gain, adapter_down_weight, adapter_up_weight):
    passed_local, grad_pair = replica_backward(
        activations[0],
        upstream[0],
        section_norm_gain[0],
        adapter_down_weight[0],
        adapter_up_weight[0],
    )
    shifted = from_behind(passed_local[None], "section", -1)
    merged_gradient = gram_adasum(grad_pair)
    return (shifted, merged_gradient)


def solution(mesh):
    sections, replicas = mesh.devices.shape
    z_size = 16 if replicas % 16 == 0 else replicas
    grid = Mesh(
        mesh.devices.reshape(sections, replicas // z_size, z_size), ("section", "y", "z")
    )
    return jax.shard_map(
        per_device,
        mesh=grid,
        in_specs=(
            P("section", ("y", "z"), None),
            P("section", ("y", "z"), None),
            P("section", None),
            P("section", None, None),
            P("section", None, None),
        ),
        out_specs=(P("section", ("y", "z"), None), P("section", ("y", "z"))),
        check_vma=False,
    )
```

```python
import numpy as np
import jax
import jax.numpy as jnp
from jax import lax
from jax.sharding import PartitionSpec as P
from jax.experimental import pallas as pl

norm_eps = 1e-05
pair_eps = 1e-06
adapter_scale = 2.0
HIGH = lax.Precision.HIGHEST


def swapped(value, axis, bit):
    mask = 2**bit
    pairs = [(source, source ^ mask) for source in range(lax.axis_size(axis))]
    return lax.ppermute(value, axis, pairs)


def from_behind(x, axis, by):
    size = lax.axis_size(axis)
    pairs = [(i, i + by) for i in range(size) if 0 <= i + by < size]
    return lax.ppermute(x, axis, pairs)


def replica_backward(inputs, incoming_gradient, gain_row, down_rows, upward_rows):
    widened = inputs.astype(jnp.float32)
    inverse = lax.rsqrt(jnp.mean(widened * widened, axis=-1, keepdims=True) + norm_eps)
    scaled = widened * inverse
    normed = (scaled * gain_row).astype(jnp.bfloat16)
    reduced_gradient = jnp.einsum(
        "sh,gh->sg", normed, down_rows, preferred_element_type=jnp.float32
    ).astype(jnp.bfloat16)
    count_of_rows = inputs.shape[0]
    upward_term = (
        adapter_scale
        * jnp.einsum(
            "tk,td->kd", reduced_gradient, incoming_gradient, preferred_element_type=jnp.float32
        )
        / count_of_rows
    )
    backward_lowrank = (
        adapter_scale
        * jnp.einsum(
            "sh,gh->sg", incoming_gradient, upward_rows, preferred_element_type=jnp.float32
        )
    ).astype(jnp.bfloat16)
    down_term = (
        jnp.einsum("tk,td->kd", backward_lowrank, normed, preferred_element_type=jnp.float32)
        / count_of_rows
    )
    back_norm = (
        jnp.einsum("tk,kd->td", backward_lowrank, down_rows, preferred_element_type=jnp.float32)
        * gain_row
    )
    centre = jnp.mean(back_norm * scaled, axis=-1, keepdims=True)
    passed = incoming_gradient.astype(jnp.float32) + inverse * (back_norm - scaled * centre)
    return (passed.astype(jnp.bfloat16), jnp.stack([down_term, upward_term]))


def swap_rows(c, level_bit):
    t, n = c.shape[0], c.shape[1]
    rest = c.shape[2:]
    g = c.reshape((t, n // 2 ** (level_bit + 1), 2, 2 ** level_bit) + rest)
    return g[:, :, ::-1].reshape(c.shape)


def coefficient_tree(gram):
    tensors, n = gram.shape[0], gram.shape[1]
    coef = jnp.broadcast_to(jnp.eye(n, dtype=jnp.float32), (tensors, n, n))
    for level_bit in range(n.bit_length() - 1):
        partner = swap_rows(coef, level_bit)
        gc = jnp.einsum("tra,tab->trb", coef, gram, precision=HIGH)
        inner_sum = jnp.sum(gc * partner, axis=-1, keepdims=True)
        own_square = jnp.sum(gc * coef, axis=-1, keepdims=True)
        far_square = swap_rows(own_square, level_bit)
        keep_coef = 1.0 - inner_sum / (2.0 * (own_square + pair_eps))
        take_coef = 1.0 - inner_sum / (2.0 * (far_square + pair_eps))
        coef = keep_coef * coef + take_coef * partner
    return coef[:, 0, :]


def bit_reversed_eye(n):
    bits = n.bit_length() - 1
    order = [int(format(i, f"0{bits}b")[::-1], 2) for i in range(n)]
    return np.eye(n, dtype=np.float32)[order]


def combine_kernel(start_ref, gram_ref, sel_ref, high_ref, low_ref, out_ref):
    n = gram_ref.shape[0]
    finals = []
    for t in range(gram_ref.shape[1] // n):
        gram = gram_ref[:, t * n:(t + 1) * n]
        coef = start_ref[...]
        while coef.shape[0] > 1:
            half = coef.shape[0] // 2
            first, second = coef[:half], coef[half:]
            g_first = jnp.dot(first, gram, precision=HIGH, preferred_element_type=jnp.float32)
            g_second = jnp.dot(second, gram, precision=HIGH, preferred_element_type=jnp.float32)
            inner_sum = jnp.sum(g_first * second, axis=1, keepdims=True)
            own_square = jnp.sum(g_first * first, axis=1, keepdims=True)
            far_square = jnp.sum(g_second * second, axis=1, keepdims=True)
            keep_coef = 1.0 - inner_sum / (2.0 * (own_square + pair_eps))
            take_coef = 1.0 - inner_sum / (2.0 * (far_square + pair_eps))
            coef = keep_coef * first + take_coef * second
        finals.append(coef)
    sel = sel_ref[0:1, 0:n]
    row = sel * finals[0] + (1.0 - sel) * finals[1]
    eye = start_ref[...] * 0.0 + (
        lax.broadcasted_iota(jnp.int32, (n, n), 0) == lax.broadcasted_iota(jnp.int32, (n, n), 1)
    ).astype(jnp.float32)
    column = lax.dot_general(
        eye, row, (((1,), (1,)), ((), ())), precision=HIGH, preferred_element_type=jnp.float32
    )
    chunks = high_ref[...].astype(jnp.float32) + low_ref[...].astype(jnp.float32)
    combined = jnp.sum(column * chunks, axis=0, keepdims=True)
    out_ref[...] = combined.astype(out_ref.dtype)


def combine(gram_rows, first_tensor, high_chunks, low_chunks, interpret=False):
    n = gram_rows.shape[0]
    sel = jnp.broadcast_to(first_tensor.astype(jnp.float32), (8, 128))
    return pl.pallas_call(
        combine_kernel,
        out_shape=jax.ShapeDtypeStruct((1, high_chunks.shape[1]), jnp.bfloat16),
        interpret=interpret,
    )(jnp.asarray(bit_reversed_eye(n)), gram_rows, sel, high_chunks, low_chunks)


def split_three(x):
    one = x.astype(jnp.bfloat16)
    rest = x - one.astype(jnp.float32)
    two = rest.astype(jnp.bfloat16)
    three = (rest - two.astype(jnp.float32)).astype(jnp.bfloat16)
    return one, two, three


def gram_adasum(grad_pair):
    devices = lax.axis_size("dp")
    me = lax.axis_index("dp")
    flat = grad_pair.reshape(devices, -1)
    width = flat.shape[1]
    high = flat.astype(jnp.bfloat16)
    low = (flat - high.astype(jnp.float32)).astype(jnp.bfloat16)
    high_chunks = lax.all_to_all(high, "dp", 0, 0, tiled=True)
    tensors = grad_pair.shape[0]
    per_tensor = devices // tensors
    mine = me // per_tensor
    n = devices
    partial = lax.dot_general(
        high_chunks, high_chunks, (((1,), (1,)), ((), ())), preferred_element_type=jnp.float32
    )
    pad = (-(width + 3 * n)) % 128
    payload = jnp.concatenate(
        [low, *split_three(partial), jnp.zeros((devices, pad), jnp.bfloat16)], axis=1
    )
    got = lax.all_to_all(payload, "dp", 0, 0, tiled=True)
    low_chunks = got[:, :width]
    pieces = got[:, width:width + 3 * n].astype(jnp.float32).reshape(devices, 3, n)
    row_parts = (pieces[:, 0] + pieces[:, 1]) + pieces[:, 2]
    rows = jnp.sum(row_parts.reshape(tensors, per_tensor, n), axis=1)
    spread = jnp.broadcast_to(rows.reshape(1, -1), (devices, tensors * n))
    gram_rows = lax.all_to_all(spread, "dp", 0, 0, tiled=True)
    return combine(gram_rows, mine == 0, high_chunks, low_chunks)


def per_device(activations, upstream, section_norm_gain, adapter_down_weight, adapter_up_weight):
    passed_local, grad_pair = replica_backward(
        activations[0],
        upstream[0],
        section_norm_gain[0],
        adapter_down_weight[0],
        adapter_up_weight[0],
    )
    shifted = from_behind(passed_local[None], "section", -1)
    merged_gradient = gram_adasum(grad_pair)
    return (shifted, merged_gradient)


def solution(mesh):
    return jax.shard_map(
        per_device,
        mesh=mesh,
        in_specs=(
            P("section", "dp", None),
            P("section", "dp", None),
            P("section", None),
            P("section", None, None),
            P("section", None, None),
        ),
        out_specs=(P("section", "dp", None), P("section", "dp")),
        check_vma=False,
    )
```

```python
import numpy as np
import jax
import jax.numpy as jnp
from jax import lax
from jax.sharding import PartitionSpec as P
from jax.experimental import pallas as pl

norm_eps = 1e-05
pair_eps = 1e-06
adapter_scale = 2.0
HIGH = lax.Precision.HIGHEST


def swapped(value, axis, bit):
    mask = 2**bit
    pairs = [(source, source ^ mask) for source in range(lax.axis_size(axis))]
    return lax.ppermute(value, axis, pairs)


def from_behind(x, axis, by):
    size = lax.axis_size(axis)
    pairs = [(i, i + by) for i in range(size) if 0 <= i + by < size]
    return lax.ppermute(x, axis, pairs)


def replica_backward(inputs, incoming_gradient, gain_row, down_rows, upward_rows):
    widened = inputs.astype(jnp.float32)
    inverse = lax.rsqrt(jnp.mean(widened * widened, axis=-1, keepdims=True) + norm_eps)
    scaled = widened * inverse
    normed = (scaled * gain_row).astype(jnp.bfloat16)
    reduced_gradient = jnp.einsum(
        "sh,gh->sg", normed, down_rows, preferred_element_type=jnp.float32
    ).astype(jnp.bfloat16)
    count_of_rows = inputs.shape[0]
    upward_term = (
        adapter_scale
        * jnp.einsum(
            "tk,td->kd", reduced_gradient, incoming_gradient, preferred_element_type=jnp.float32
        )
        / count_of_rows
    )
    backward_lowrank = (
        adapter_scale
        * jnp.einsum(
            "sh,gh->sg", incoming_gradient, upward_rows, preferred_element_type=jnp.float32
        )
    ).astype(jnp.bfloat16)
    down_term = (
        jnp.einsum("tk,td->kd", backward_lowrank, normed, preferred_element_type=jnp.float32)
        / count_of_rows
    )
    back_norm = (
        jnp.einsum("tk,kd->td", backward_lowrank, down_rows, preferred_element_type=jnp.float32)
        * gain_row
    )
    centre = jnp.mean(back_norm * scaled, axis=-1, keepdims=True)
    passed = incoming_gradient.astype(jnp.float32) + inverse * (back_norm - scaled * centre)
    return (passed.astype(jnp.bfloat16), jnp.stack([down_term, upward_term]))


def swap_rows(c, level_bit):
    t, n = c.shape[0], c.shape[1]
    rest = c.shape[2:]
    g = c.reshape((t, n // 2 ** (level_bit + 1), 2, 2 ** level_bit) + rest)
    return g[:, :, ::-1].reshape(c.shape)


def coefficient_tree(gram):
    tensors, n = gram.shape[0], gram.shape[1]
    coef = jnp.broadcast_to(jnp.eye(n, dtype=jnp.float32), (tensors, n, n))
    for level_bit in range(n.bit_length() - 1):
        partner = swap_rows(coef, level_bit)
        gc = jnp.einsum("tra,tab->trb", coef, gram, precision=HIGH)
        inner_sum = jnp.sum(gc * partner, axis=-1, keepdims=True)
        own_square = jnp.sum(gc * coef, axis=-1, keepdims=True)
        far_square = swap_rows(own_square, level_bit)
        keep_coef = 1.0 - inner_sum / (2.0 * (own_square + pair_eps))
        take_coef = 1.0 - inner_sum / (2.0 * (far_square + pair_eps))
        coef = keep_coef * coef + take_coef * partner
    return coef[:, 0, :]


def bit_reversed_eye(n):
    bits = n.bit_length() - 1
    order = [int(format(i, f"0{bits}b")[::-1], 2) for i in range(n)]
    return np.eye(n, dtype=np.float32)[order]


def combine_kernel(start_ref, gram_ref, sel_ref, high_ref, low_ref, out_ref):
    n = gram_ref.shape[0]
    finals = []
    for t in range(gram_ref.shape[1] // n):
        gram = gram_ref[:, t * n:(t + 1) * n]
        coef = start_ref[...]
        while coef.shape[0] > 1:
            half = coef.shape[0] // 2
            first, second = coef[:half], coef[half:]
            g_first = jnp.dot(first, gram, precision=HIGH, preferred_element_type=jnp.float32)
            g_second = jnp.dot(second, gram, precision=HIGH, preferred_element_type=jnp.float32)
            inner_sum = jnp.sum(g_first * second, axis=1, keepdims=True)
            own_square = jnp.sum(g_first * first, axis=1, keepdims=True)
            far_square = jnp.sum(g_second * second, axis=1, keepdims=True)
            keep_coef = 1.0 - inner_sum / (2.0 * (own_square + pair_eps))
            take_coef = 1.0 - inner_sum / (2.0 * (far_square + pair_eps))
            coef = keep_coef * first + take_coef * second
        finals.append(coef)
    sel = sel_ref[0:1, 0:n]
    row = sel * finals[0] + (1.0 - sel) * finals[1]
    eye = start_ref[...] * 0.0 + (
        lax.broadcasted_iota(jnp.int32, (n, n), 0) == lax.broadcasted_iota(jnp.int32, (n, n), 1)
    ).astype(jnp.float32)
    column = lax.dot_general(
        eye, row, (((1,), (1,)), ((), ())), precision=HIGH, preferred_element_type=jnp.float32
    )
    width = high_ref.shape[1]
    chunks = high_ref[...].astype(jnp.float32) + low_ref[:, 0:width].astype(jnp.float32)
    combined = jnp.sum(column * chunks, axis=0, keepdims=True)
    out_ref[...] = combined.astype(out_ref.dtype)


def combine(gram_rows, first_tensor, high_chunks, low_chunks, interpret=False):
    n = gram_rows.shape[0]
    sel = jnp.broadcast_to(first_tensor.astype(jnp.float32), (8, 128))
    return pl.pallas_call(
        combine_kernel,
        out_shape=jax.ShapeDtypeStruct((1, high_chunks.shape[1]), jnp.bfloat16),
        interpret=interpret,
    )(jnp.asarray(bit_reversed_eye(n)), gram_rows, sel, high_chunks, low_chunks)


def to_bf16_grid(x):
    return lax.reduce_precision(x, exponent_bits=8, mantissa_bits=7)


def split_three(x):
    one = to_bf16_grid(x)
    rest = x - one
    two = to_bf16_grid(rest)
    three = rest - two
    return [part.astype(jnp.bfloat16) for part in (one, two, three)]


def gram_adasum(grad_pair):
    devices = lax.axis_size("dp")
    me = lax.axis_index("dp")
    flat = grad_pair.reshape(devices, -1)
    width = flat.shape[1]
    high_grid = to_bf16_grid(flat)
    high = high_grid.astype(jnp.bfloat16)
    low = (flat - high_grid).astype(jnp.bfloat16)
    high_chunks = lax.all_to_all(high, "dp", 0, 0, tiled=True)
    tensors = grad_pair.shape[0]
    per_tensor = devices // tensors
    mine = me // per_tensor
    n = devices
    partial = lax.dot_general(
        high_chunks, high_chunks, (((1,), (1,)), ((), ())), preferred_element_type=jnp.float32
    )
    pad = (-(width + 3 * n)) % 128
    payload = jnp.concatenate(
        [low, *split_three(partial), jnp.zeros((devices, pad), jnp.bfloat16)], axis=1
    )
    got = lax.all_to_all(payload, "dp", 0, 0, tiled=True)
    pieces = got[:, width:width + 3 * n].astype(jnp.float32).reshape(devices, 3, n)
    row_parts = (pieces[:, 0] + pieces[:, 1]) + pieces[:, 2]
    rows = jnp.sum(row_parts.reshape(tensors, per_tensor, n), axis=1)
    spread = jnp.broadcast_to(rows.reshape(1, -1), (devices, tensors * n))
    gram_rows = lax.all_to_all(spread, "dp", 0, 0, tiled=True)
    return combine(gram_rows, mine == 0, high_chunks, got)


def per_device(activations, upstream, section_norm_gain, adapter_down_weight, adapter_up_weight):
    passed_local, grad_pair = replica_backward(
        activations[0],
        upstream[0],
        section_norm_gain[0],
        adapter_down_weight[0],
        adapter_up_weight[0],
    )
    shifted = from_behind(passed_local[None], "section", -1)
    merged_gradient = gram_adasum(grad_pair)
    return (shifted, merged_gradient)


def solution(mesh):
    return jax.shard_map(
        per_device,
        mesh=mesh,
        in_specs=(
            P("section", "dp", None),
            P("section", "dp", None),
            P("section", None),
            P("section", None, None),
            P("section", None, None),
        ),
        out_specs=(P("section", "dp", None), P("section", "dp")),
        check_vma=False,
    )
```

```python
import numpy as np
import jax
import jax.numpy as jnp
from jax import lax
from jax.sharding import PartitionSpec as P
from jax.experimental import pallas as pl

norm_eps = 1e-05
pair_eps = 1e-06
adapter_scale = 2.0
HIGH = lax.Precision.HIGHEST


def swapped(value, axis, bit):
    mask = 2**bit
    pairs = [(source, source ^ mask) for source in range(lax.axis_size(axis))]
    return lax.ppermute(value, axis, pairs)


def from_behind(x, axis, by):
    size = lax.axis_size(axis)
    pairs = [(i, i + by) for i in range(size) if 0 <= i + by < size]
    return lax.ppermute(x, axis, pairs)


def replica_backward(inputs, incoming_gradient, gain_row, down_rows, upward_rows):
    widened = inputs.astype(jnp.float32)
    inverse = lax.rsqrt(jnp.mean(widened * widened, axis=-1, keepdims=True) + norm_eps)
    scaled = widened * inverse
    normed = (scaled * gain_row).astype(jnp.bfloat16)
    reduced_gradient = jnp.einsum(
        "sh,gh->sg", normed, down_rows, preferred_element_type=jnp.float32
    ).astype(jnp.bfloat16)
    count_of_rows = inputs.shape[0]
    upward_term = (
        adapter_scale
        * jnp.einsum(
            "tk,td->kd", reduced_gradient, incoming_gradient, preferred_element_type=jnp.float32
        )
        / count_of_rows
    )
    backward_lowrank = (
        adapter_scale
        * jnp.einsum(
            "sh,gh->sg", incoming_gradient, upward_rows, preferred_element_type=jnp.float32
        )
    ).astype(jnp.bfloat16)
    down_term = (
        jnp.einsum("tk,td->kd", backward_lowrank, normed, preferred_element_type=jnp.float32)
        / count_of_rows
    )
    back_norm = (
        jnp.einsum("tk,kd->td", backward_lowrank, down_rows, preferred_element_type=jnp.float32)
        * gain_row
    )
    centre = jnp.mean(back_norm * scaled, axis=-1, keepdims=True)
    passed = incoming_gradient.astype(jnp.float32) + inverse * (back_norm - scaled * centre)
    return (passed.astype(jnp.bfloat16), jnp.stack([down_term, upward_term]))


def swap_rows(c, level_bit):
    t, n = c.shape[0], c.shape[1]
    rest = c.shape[2:]
    g = c.reshape((t, n // 2 ** (level_bit + 1), 2, 2 ** level_bit) + rest)
    return g[:, :, ::-1].reshape(c.shape)


def coefficient_tree(gram):
    tensors, n = gram.shape[0], gram.shape[1]
    coef = jnp.broadcast_to(jnp.eye(n, dtype=jnp.float32), (tensors, n, n))
    for level_bit in range(n.bit_length() - 1):
        partner = swap_rows(coef, level_bit)
        gc = jnp.einsum("tra,tab->trb", coef, gram, precision=HIGH)
        inner_sum = jnp.sum(gc * partner, axis=-1, keepdims=True)
        own_square = jnp.sum(gc * coef, axis=-1, keepdims=True)
        far_square = swap_rows(own_square, level_bit)
        keep_coef = 1.0 - inner_sum / (2.0 * (own_square + pair_eps))
        take_coef = 1.0 - inner_sum / (2.0 * (far_square + pair_eps))
        coef = keep_coef * coef + take_coef * partner
    return coef[:, 0, :]


def bit_reversed_eye(n):
    bits = n.bit_length() - 1
    order = [int(format(i, f"0{bits}b")[::-1], 2) for i in range(n)]
    return np.eye(n, dtype=np.float32)[order]


def combine_kernel(start_ref, gram_ref, chunks_ref, out_ref):
    n = gram_ref.shape[0]
    finals = []
    for t in range(gram_ref.shape[1] // n):
        gram = gram_ref[:, t * n:(t + 1) * n]
        coef = start_ref[...]
        while coef.shape[0] > 1:
            half = coef.shape[0] // 2
            first, second = coef[:half], coef[half:]
            g_first = jnp.dot(first, gram, precision=HIGH, preferred_element_type=jnp.float32)
            g_second = jnp.dot(second, gram, precision=HIGH, preferred_element_type=jnp.float32)
            inner_sum = jnp.sum(g_first * second, axis=1, keepdims=True)
            own_square = jnp.sum(g_first * first, axis=1, keepdims=True)
            far_square = jnp.sum(g_second * second, axis=1, keepdims=True)
            keep_coef = 1.0 - inner_sum / (2.0 * (own_square + pair_eps))
            take_coef = 1.0 - inner_sum / (2.0 * (far_square + pair_eps))
            coef = keep_coef * first + take_coef * second
        finals.append(coef)
    sel = jnp.where(lax.axis_index("dp") < lax.axis_size("dp") // 2, 1.0, 0.0)
    row = sel * finals[0] + (1.0 - sel) * finals[1]
    eye = start_ref[...] * 0.0 + (
        lax.broadcasted_iota(jnp.int32, (n, n), 0) == lax.broadcasted_iota(jnp.int32, (n, n), 1)
    ).astype(jnp.float32)
    column = lax.dot_general(
        eye, row, (((1,), (1,)), ((), ())), precision=HIGH, preferred_element_type=jnp.float32
    )
    combined = jnp.sum(column * chunks_ref[...], axis=0, keepdims=True)
    out_ref[...] = combined.astype(out_ref.dtype)


def combine(gram_rows, chunks, interpret=False):
    n = gram_rows.shape[0]
    return pl.pallas_call(
        combine_kernel,
        out_shape=jax.ShapeDtypeStruct((1, chunks.shape[1]), jnp.bfloat16),
        interpret=interpret,
    )(jnp.asarray(bit_reversed_eye(n)), gram_rows, chunks)


def gram_adasum(grad_pair, passed):
    devices = lax.axis_size("dp")
    me = lax.axis_index("dp")
    flat = grad_pair.reshape(devices, -1)
    chunks = lax.all_to_all(flat, "dp", 0, 0, tiled=True)
    tensors = grad_pair.shape[0]
    per_tensor = devices // tensors
    mine = me // per_tensor
    partial = jnp.dot(chunks, chunks.T, precision=HIGH, preferred_element_type=jnp.float32)
    rows = lax.all_to_all(partial[:, None, :], "dp", 0, 0, tiled=True)
    rows = jnp.sum(rows.reshape(tensors, per_tensor, partial.shape[1]), axis=1)
    spread = jnp.broadcast_to(rows.reshape(1, -1), (devices, tensors * partial.shape[1]))
    spread, passed = lax.optimization_barrier((spread, passed))
    has_next = lax.axis_index("section") < lax.axis_size("section") - 1
    passed = jnp.where(has_next, passed, jnp.zeros_like(passed))
    gram_rows = lax.all_to_all(spread, "dp", 0, 0, tiled=True)
    return combine(gram_rows, chunks), passed


def per_device(activations, upstream, section_norm_gain, adapter_down_weight, adapter_up_weight):
    passed_local, grad_pair = replica_backward(
        activations[0],
        upstream[0],
        section_norm_gain[0],
        adapter_down_weight[0],
        adapter_up_weight[0],
    )
    shifted = from_behind(passed_local[None], "section", -1)
    merged_gradient, shifted = gram_adasum(grad_pair, shifted)
    return (shifted, merged_gradient)


def solution(mesh):
    return jax.shard_map(
        per_device,
        mesh=mesh,
        in_specs=(
            P("section", "dp", None),
            P("section", "dp", None),
            P("section", None),
            P("section", None, None),
            P("section", None, None),
        ),
        out_specs=(P("section", "dp", None), P("section", "dp")),
        check_vma=False,
    )
```

```python
import numpy as np
import jax
import jax.numpy as jnp
from jax import lax
from jax.sharding import PartitionSpec as P
from jax.experimental import pallas as pl

norm_eps = 1e-05
pair_eps = 1e-06
adapter_scale = 2.0
HIGH = lax.Precision.HIGHEST


def swapped(value, axis, bit):
    mask = 2**bit
    pairs = [(source, source ^ mask) for source in range(lax.axis_size(axis))]
    return lax.ppermute(value, axis, pairs)


def from_behind(x, axis, by):
    size = lax.axis_size(axis)
    pairs = [(i, i + by) for i in range(size) if 0 <= i + by < size]
    return lax.ppermute(x, axis, pairs)


def replica_backward(inputs, incoming_gradient, gain_row, down_rows, upward_rows):
    widened = inputs.astype(jnp.float32)
    inverse = lax.rsqrt(jnp.mean(widened * widened, axis=-1, keepdims=True) + norm_eps)
    scaled = widened * inverse
    normed = (scaled * gain_row).astype(jnp.bfloat16)
    reduced_gradient = jnp.einsum(
        "sh,gh->sg", normed, down_rows, preferred_element_type=jnp.float32
    ).astype(jnp.bfloat16)
    count_of_rows = inputs.shape[0]
    upward_term = (
        adapter_scale
        * jnp.einsum(
            "tk,td->kd", reduced_gradient, incoming_gradient, preferred_element_type=jnp.float32
        )
        / count_of_rows
    )
    backward_lowrank = (
        adapter_scale
        * jnp.einsum(
            "sh,gh->sg", incoming_gradient, upward_rows, preferred_element_type=jnp.float32
        )
    ).astype(jnp.bfloat16)
    down_term = (
        jnp.einsum("tk,td->kd", backward_lowrank, normed, preferred_element_type=jnp.float32)
        / count_of_rows
    )
    back_norm = (
        jnp.einsum("tk,kd->td", backward_lowrank, down_rows, preferred_element_type=jnp.float32)
        * gain_row
    )
    centre = jnp.mean(back_norm * scaled, axis=-1, keepdims=True)
    passed = incoming_gradient.astype(jnp.float32) + inverse * (back_norm - scaled * centre)
    return (passed.astype(jnp.bfloat16), jnp.stack([down_term, upward_term]))


def swap_rows(c, level_bit):
    t, n = c.shape[0], c.shape[1]
    rest = c.shape[2:]
    g = c.reshape((t, n // 2 ** (level_bit + 1), 2, 2 ** level_bit) + rest)
    return g[:, :, ::-1].reshape(c.shape)


def coefficient_tree(gram):
    tensors, n = gram.shape[0], gram.shape[1]
    coef = jnp.broadcast_to(jnp.eye(n, dtype=jnp.float32), (tensors, n, n))
    for level_bit in range(n.bit_length() - 1):
        partner = swap_rows(coef, level_bit)
        gc = jnp.einsum("tra,tab->trb", coef, gram, precision=HIGH)
        inner_sum = jnp.sum(gc * partner, axis=-1, keepdims=True)
        own_square = jnp.sum(gc * coef, axis=-1, keepdims=True)
        far_square = swap_rows(own_square, level_bit)
        keep_coef = 1.0 - inner_sum / (2.0 * (own_square + pair_eps))
        take_coef = 1.0 - inner_sum / (2.0 * (far_square + pair_eps))
        coef = keep_coef * coef + take_coef * partner
    return coef[:, 0, :]


def pair_kernel(x_ref, g_ref, gain_ref, down_ref, up_ref, out_ref):
    widened = x_ref[...].astype(jnp.float32)
    width = widened.shape[1]
    rows = widened.shape[0]
    inverse = lax.rsqrt(jnp.sum(widened * widened, axis=1, keepdims=True) / width + norm_eps)
    normed = (widened * inverse * gain_ref[...]).astype(jnp.bfloat16)
    contract_last = (((1,), (1,)), ((), ()))
    contract_first = (((0,), (0,)), ((), ()))
    reduced = lax.dot_general(
        normed, down_ref[...], contract_last, preferred_element_type=jnp.float32
    ).astype(jnp.bfloat16)
    incoming = g_ref[...]
    out_ref[1] = (
        adapter_scale
        * lax.dot_general(reduced, incoming, contract_first, preferred_element_type=jnp.float32)
        / rows
    )
    backward_lowrank = (
        adapter_scale
        * lax.dot_general(incoming, up_ref[...], contract_last, preferred_element_type=jnp.float32)
    ).astype(jnp.bfloat16)
    out_ref[0] = (
        lax.dot_general(backward_lowrank, normed, contract_first, preferred_element_type=jnp.float32)
        / rows
    )


def gradient_pair(inputs, incoming_gradient, gain_row, down_rows, upward_rows, interpret=False):
    rank, width = down_rows.shape
    return pl.pallas_call(
        pair_kernel,
        out_shape=jax.ShapeDtypeStruct((2, rank, width), jnp.float32),
        interpret=interpret,
    )(inputs, incoming_gradient, gain_row[None], down_rows, upward_rows)


def bit_reversed_eye(n):
    bits = n.bit_length() - 1
    order = [int(format(i, f"0{bits}b")[::-1], 2) for i in range(n)]
    return np.eye(n, dtype=np.float32)[order]


def combine_kernel(start_ref, gram_ref, sel_ref, chunks_ref, out_ref):
    n = gram_ref.shape[0]
    finals = []
    for t in range(gram_ref.shape[1] // n):
        gram = gram_ref[:, t * n:(t + 1) * n]
        coef = start_ref[...]
        while coef.shape[0] > 1:
            half = coef.shape[0] // 2
            first, second = coef[:half], coef[half:]
            g_first = jnp.dot(first, gram, precision=HIGH, preferred_element_type=jnp.float32)
            g_second = jnp.dot(second, gram, precision=HIGH, preferred_element_type=jnp.float32)
            inner_sum = jnp.sum(g_first * second, axis=1, keepdims=True)
            own_square = jnp.sum(g_first * first, axis=1, keepdims=True)
            far_square = jnp.sum(g_second * second, axis=1, keepdims=True)
            keep_coef = 1.0 - inner_sum / (2.0 * (own_square + pair_eps))
            take_coef = 1.0 - inner_sum / (2.0 * (far_square + pair_eps))
            coef = keep_coef * first + take_coef * second
        finals.append(coef)
    sel = sel_ref[0:1, 0:n]
    row = sel * finals[0] + (1.0 - sel) * finals[1]
    eye = start_ref[...] * 0.0 + (
        lax.broadcasted_iota(jnp.int32, (n, n), 0) == lax.broadcasted_iota(jnp.int32, (n, n), 1)
    ).astype(jnp.float32)
    column = lax.dot_general(
        eye, row, (((1,), (1,)), ((), ())), precision=HIGH, preferred_element_type=jnp.float32
    )
    combined = jnp.sum(column * chunks_ref[...], axis=0, keepdims=True)
    out_ref[...] = combined.astype(out_ref.dtype)


def combine(gram_rows, first_tensor, chunks, interpret=False):
    n = gram_rows.shape[0]
    sel = jnp.broadcast_to(first_tensor.astype(jnp.float32), (8, 128))
    return pl.pallas_call(
        combine_kernel,
        out_shape=jax.ShapeDtypeStruct((1, chunks.shape[1]), jnp.bfloat16),
        interpret=interpret,
    )(jnp.asarray(bit_reversed_eye(n)), gram_rows, sel, chunks)


def gram_adasum(grad_pair):
    devices = lax.axis_size("dp")
    me = lax.axis_index("dp")
    flat = grad_pair.reshape(devices, -1)
    chunks = lax.all_to_all(flat, "dp", 0, 0, tiled=True)
    tensors = grad_pair.shape[0]
    per_tensor = devices // tensors
    mine = me // per_tensor
    partial = jnp.dot(chunks, chunks.T, precision=HIGH, preferred_element_type=jnp.float32)
    rows = lax.all_to_all(partial[:, None, :], "dp", 0, 0, tiled=True)
    rows = jnp.sum(rows.reshape(tensors, per_tensor, partial.shape[1]), axis=1)
    spread = jnp.broadcast_to(rows.reshape(1, -1), (devices, tensors * partial.shape[1]))
    gram_rows = lax.all_to_all(spread, "dp", 0, 0, tiled=True)
    return combine(gram_rows, mine == 0, chunks)


def per_device(activations, upstream, section_norm_gain, adapter_down_weight, adapter_up_weight):
    passed_local, grad_pair = replica_backward(
        activations[0],
        upstream[0],
        section_norm_gain[0],
        adapter_down_weight[0],
        adapter_up_weight[0],
    )
    grad_pair = gradient_pair(
        activations[0],
        upstream[0],
        section_norm_gain[0],
        adapter_down_weight[0],
        adapter_up_weight[0],
    )
    shifted = from_behind(passed_local[None], "section", -1)
    merged_gradient = gram_adasum(grad_pair)
    return (shifted, merged_gradient)


def solution(mesh):
    return jax.shard_map(
        per_device,
        mesh=mesh,
        in_specs=(
            P("section", "dp", None),
            P("section", "dp", None),
            P("section", None),
            P("section", None, None),
            P("section", None, None),
        ),
        out_specs=(P("section", "dp", None), P("section", "dp")),
        check_vma=False,
    )
```

```python
import numpy as np
import jax
import jax.numpy as jnp
from jax import lax
from jax.sharding import PartitionSpec as P
from jax.experimental import pallas as pl

norm_eps = 1e-05
pair_eps = 1e-06
adapter_scale = 2.0
HIGH = lax.Precision.HIGHEST


def swapped(value, axis, bit):
    mask = 2**bit
    pairs = [(source, source ^ mask) for source in range(lax.axis_size(axis))]
    return lax.ppermute(value, axis, pairs)


def from_behind(x, axis, by):
    size = lax.axis_size(axis)
    pairs = [(i, i + by) for i in range(size) if 0 <= i + by < size]
    return lax.ppermute(x, axis, pairs)


def replica_backward(inputs, incoming_gradient, gain_row, down_rows, upward_rows):
    widened = inputs.astype(jnp.float32)
    inverse = lax.rsqrt(jnp.mean(widened * widened, axis=-1, keepdims=True) + norm_eps)
    scaled = widened * inverse
    normed = (scaled * gain_row).astype(jnp.bfloat16)
    reduced_gradient = jnp.einsum(
        "sh,gh->sg", normed, down_rows, preferred_element_type=jnp.float32
    ).astype(jnp.bfloat16)
    count_of_rows = inputs.shape[0]
    upward_term = (
        adapter_scale
        * jnp.einsum(
            "tk,td->kd", reduced_gradient, incoming_gradient, preferred_element_type=jnp.float32
        )
        / count_of_rows
    )
    backward_lowrank = (
        adapter_scale
        * jnp.einsum(
            "sh,gh->sg", incoming_gradient, upward_rows, preferred_element_type=jnp.float32
        )
    ).astype(jnp.bfloat16)
    down_term = (
        jnp.einsum("tk,td->kd", backward_lowrank, normed, preferred_element_type=jnp.float32)
        / count_of_rows
    )
    back_norm = (
        jnp.einsum("tk,kd->td", backward_lowrank, down_rows, preferred_element_type=jnp.float32)
        * gain_row
    )
    centre = jnp.mean(back_norm * scaled, axis=-1, keepdims=True)
    passed = incoming_gradient.astype(jnp.float32) + inverse * (back_norm - scaled * centre)
    return (passed.astype(jnp.bfloat16), jnp.stack([down_term, upward_term]))


def swap_rows(c, level_bit):
    t, n = c.shape[0], c.shape[1]
    rest = c.shape[2:]
    g = c.reshape((t, n // 2 ** (level_bit + 1), 2, 2 ** level_bit) + rest)
    return g[:, :, ::-1].reshape(c.shape)


def coefficient_tree(gram):
    tensors, n = gram.shape[0], gram.shape[1]
    coef = jnp.broadcast_to(jnp.eye(n, dtype=jnp.float32), (tensors, n, n))
    for level_bit in range(n.bit_length() - 1):
        partner = swap_rows(coef, level_bit)
        gc = jnp.einsum("tra,tab->trb", coef, gram, precision=HIGH)
        inner_sum = jnp.sum(gc * partner, axis=-1, keepdims=True)
        own_square = jnp.sum(gc * coef, axis=-1, keepdims=True)
        far_square = swap_rows(own_square, level_bit)
        keep_coef = 1.0 - inner_sum / (2.0 * (own_square + pair_eps))
        take_coef = 1.0 - inner_sum / (2.0 * (far_square + pair_eps))
        coef = keep_coef * coef + take_coef * partner
    return coef[:, 0, :]


def pair_kernel(x_ref, g_ref, gain_ref, down_ref, up_ref, out_ref):
    widened = x_ref[...].astype(jnp.float32)
    width = widened.shape[1]
    rows = widened.shape[0]
    inverse = lax.rsqrt(jnp.sum(widened * widened, axis=1, keepdims=True) / width + norm_eps)
    normed = (widened * inverse * gain_ref[...]).astype(jnp.bfloat16)
    contract_last = (((1,), (1,)), ((), ()))
    incoming = g_ref[...]
    reduced_t = lax.dot_general(
        down_ref[...], normed, contract_last, preferred_element_type=jnp.float32
    ).astype(jnp.bfloat16)
    out_ref[1] = (
        adapter_scale * jnp.dot(reduced_t, incoming, preferred_element_type=jnp.float32) / rows
    )
    backward_lowrank_t = (
        adapter_scale
        * lax.dot_general(up_ref[...], incoming, contract_last, preferred_element_type=jnp.float32)
    ).astype(jnp.bfloat16)
    out_ref[0] = jnp.dot(backward_lowrank_t, normed, preferred_element_type=jnp.float32) / rows


def gradient_pair(inputs, incoming_gradient, gain_row, down_rows, upward_rows, interpret=False):
    rank, width = down_rows.shape
    return pl.pallas_call(
        pair_kernel,
        out_shape=jax.ShapeDtypeStruct((2, rank, width), jnp.float32),
        interpret=interpret,
    )(inputs, incoming_gradient, gain_row[None], down_rows, upward_rows)


def bit_reversed_eye(n):
    bits = n.bit_length() - 1
    order = [int(format(i, f"0{bits}b")[::-1], 2) for i in range(n)]
    return np.eye(n, dtype=np.float32)[order]


def combine_kernel(start_ref, gram_ref, sel_ref, chunks_ref, out_ref):
    n = gram_ref.shape[0]
    finals = []
    for t in range(gram_ref.shape[1] // n):
        gram = gram_ref[:, t * n:(t + 1) * n]
        coef = start_ref[...]
        while coef.shape[0] > 1:
            half = coef.shape[0] // 2
            first, second = coef[:half], coef[half:]
            g_first = jnp.dot(first, gram, precision=HIGH, preferred_element_type=jnp.float32)
            g_second = jnp.dot(second, gram, precision=HIGH, preferred_element_type=jnp.float32)
            inner_sum = jnp.sum(g_first * second, axis=1, keepdims=True)
            own_square = jnp.sum(g_first * first, axis=1, keepdims=True)
            far_square = jnp.sum(g_second * second, axis=1, keepdims=True)
            keep_coef = 1.0 - inner_sum / (2.0 * (own_square + pair_eps))
            take_coef = 1.0 - inner_sum / (2.0 * (far_square + pair_eps))
            coef = keep_coef * first + take_coef * second
        finals.append(coef)
    sel = sel_ref[0:1, 0:n]
    row = sel * finals[0] + (1.0 - sel) * finals[1]
    eye = start_ref[...] * 0.0 + (
        lax.broadcasted_iota(jnp.int32, (n, n), 0) == lax.broadcasted_iota(jnp.int32, (n, n), 1)
    ).astype(jnp.float32)
    column = lax.dot_general(
        eye, row, (((1,), (1,)), ((), ())), precision=HIGH, preferred_element_type=jnp.float32
    )
    combined = jnp.sum(column * chunks_ref[...], axis=0, keepdims=True)
    out_ref[...] = combined.astype(out_ref.dtype)


def combine(gram_rows, first_tensor, chunks, interpret=False):
    n = gram_rows.shape[0]
    sel = jnp.broadcast_to(first_tensor.astype(jnp.float32), (8, 128))
    return pl.pallas_call(
        combine_kernel,
        out_shape=jax.ShapeDtypeStruct((1, chunks.shape[1]), jnp.bfloat16),
        interpret=interpret,
    )(jnp.asarray(bit_reversed_eye(n)), gram_rows, sel, chunks)


def gram_adasum(grad_pair):
    devices = lax.axis_size("dp")
    me = lax.axis_index("dp")
    flat = grad_pair.reshape(devices, -1)
    chunks = lax.all_to_all(flat, "dp", 0, 0, tiled=True)
    tensors = grad_pair.shape[0]
    per_tensor = devices // tensors
    mine = me // per_tensor
    partial = jnp.dot(chunks, chunks.T, precision=HIGH, preferred_element_type=jnp.float32)
    rows = lax.all_to_all(partial[:, None, :], "dp", 0, 0, tiled=True)
    rows = jnp.sum(rows.reshape(tensors, per_tensor, partial.shape[1]), axis=1)
    spread = jnp.broadcast_to(rows.reshape(1, -1), (devices, tensors * partial.shape[1]))
    gram_rows = lax.all_to_all(spread, "dp", 0, 0, tiled=True)
    return combine(gram_rows, mine == 0, chunks)


def per_device(activations, upstream, section_norm_gain, adapter_down_weight, adapter_up_weight):
    passed_local, grad_pair = replica_backward(
        activations[0],
        upstream[0],
        section_norm_gain[0],
        adapter_down_weight[0],
        adapter_up_weight[0],
    )
    grad_pair = gradient_pair(
        activations[0],
        upstream[0],
        section_norm_gain[0],
        adapter_down_weight[0],
        adapter_up_weight[0],
    )
    shifted = from_behind(passed_local[None], "section", -1)
    merged_gradient = gram_adasum(grad_pair)
    return (shifted, merged_gradient)


def solution(mesh):
    return jax.shard_map(
        per_device,
        mesh=mesh,
        in_specs=(
            P("section", "dp", None),
            P("section", "dp", None),
            P("section", None),
            P("section", None, None),
            P("section", None, None),
        ),
        out_specs=(P("section", "dp", None), P("section", "dp")),
        check_vma=False,
    )
```

```python
import numpy as np
import jax
import jax.numpy as jnp
from jax import lax
from jax.sharding import PartitionSpec as P
from jax.experimental import pallas as pl

norm_eps = 1e-05
pair_eps = 1e-06
adapter_scale = 2.0
HIGH = lax.Precision.HIGHEST


def swapped(value, axis, bit):
    mask = 2**bit
    pairs = [(source, source ^ mask) for source in range(lax.axis_size(axis))]
    return lax.ppermute(value, axis, pairs)


def from_behind(x, axis, by):
    size = lax.axis_size(axis)
    pairs = [(i, i + by) for i in range(size) if 0 <= i + by < size]
    return lax.ppermute(x, axis, pairs)


def replica_backward(inputs, incoming_gradient, gain_row, down_rows, upward_rows):
    widened = inputs.astype(jnp.float32)
    inverse = lax.rsqrt(jnp.mean(widened * widened, axis=-1, keepdims=True) + norm_eps)
    scaled = widened * inverse
    normed = (scaled * gain_row).astype(jnp.bfloat16)
    reduced_gradient = jnp.einsum(
        "sh,gh->sg", normed, down_rows, preferred_element_type=jnp.float32
    ).astype(jnp.bfloat16)
    count_of_rows = inputs.shape[0]
    upward_term = (
        adapter_scale
        * jnp.einsum(
            "tk,td->kd", reduced_gradient, incoming_gradient, preferred_element_type=jnp.float32
        )
        / count_of_rows
    )
    backward_lowrank = (
        adapter_scale
        * jnp.einsum(
            "sh,gh->sg", incoming_gradient, upward_rows, preferred_element_type=jnp.float32
        )
    ).astype(jnp.bfloat16)
    down_term = (
        jnp.einsum("tk,td->kd", backward_lowrank, normed, preferred_element_type=jnp.float32)
        / count_of_rows
    )
    back_norm = (
        jnp.einsum("tk,kd->td", backward_lowrank, down_rows, preferred_element_type=jnp.float32)
        * gain_row
    )
    centre = jnp.mean(back_norm * scaled, axis=-1, keepdims=True)
    passed = incoming_gradient.astype(jnp.float32) + inverse * (back_norm - scaled * centre)
    return (passed.astype(jnp.bfloat16), jnp.stack([down_term, upward_term]))


def swap_rows(c, level_bit):
    t, n = c.shape[0], c.shape[1]
    rest = c.shape[2:]
    g = c.reshape((t, n // 2 ** (level_bit + 1), 2, 2 ** level_bit) + rest)
    return g[:, :, ::-1].reshape(c.shape)


def coefficient_tree(gram):
    tensors, n = gram.shape[0], gram.shape[1]
    coef = jnp.broadcast_to(jnp.eye(n, dtype=jnp.float32), (tensors, n, n))
    for level_bit in range(n.bit_length() - 1):
        partner = swap_rows(coef, level_bit)
        gc = jnp.einsum("tra,tab->trb", coef, gram, precision=HIGH)
        inner_sum = jnp.sum(gc * partner, axis=-1, keepdims=True)
        own_square = jnp.sum(gc * coef, axis=-1, keepdims=True)
        far_square = swap_rows(own_square, level_bit)
        keep_coef = 1.0 - inner_sum / (2.0 * (own_square + pair_eps))
        take_coef = 1.0 - inner_sum / (2.0 * (far_square + pair_eps))
        coef = keep_coef * coef + take_coef * partner
    return coef[:, 0, :]


def bit_reversed_eye(n):
    bits = n.bit_length() - 1
    order = [int(format(i, f"0{bits}b")[::-1], 2) for i in range(n)]
    return np.eye(n, dtype=np.float32)[order]


def combine_kernel(start_ref, gram_ref, chunks_ref, out_ref):
    n = gram_ref.shape[0]
    first_tensor = lax.axis_index("dp") < lax.axis_size("dp") // 2
    gram = jnp.where(first_tensor, gram_ref[:, 0:n], gram_ref[:, n:2 * n])
    coef = start_ref[...]
    while coef.shape[0] > 1:
        half = coef.shape[0] // 2
        first, second = coef[:half], coef[half:]
        g_first = jnp.dot(first, gram, precision=HIGH, preferred_element_type=jnp.float32)
        g_second = jnp.dot(second, gram, precision=HIGH, preferred_element_type=jnp.float32)
        inner_sum = jnp.sum(g_first * second, axis=1, keepdims=True)
        own_square = jnp.sum(g_first * first, axis=1, keepdims=True)
        far_square = jnp.sum(g_second * second, axis=1, keepdims=True)
        keep_coef = 1.0 - inner_sum / (2.0 * (own_square + pair_eps))
        take_coef = 1.0 - inner_sum / (2.0 * (far_square + pair_eps))
        coef = keep_coef * first + take_coef * second
    eye = (
        lax.broadcasted_iota(jnp.int32, (n, n), 0) == lax.broadcasted_iota(jnp.int32, (n, n), 1)
    ).astype(jnp.float32)
    column = lax.dot_general(
        eye, coef, (((1,), (1,)), ((), ())), precision=HIGH, preferred_element_type=jnp.float32
    )
    combined = jnp.sum(column * chunks_ref[...], axis=0, keepdims=True)
    out_ref[...] = combined.astype(out_ref.dtype)


def combine(gram_rows, chunks, interpret=False):
    n = gram_rows.shape[0]
    return pl.pallas_call(
        combine_kernel,
        out_shape=jax.ShapeDtypeStruct((1, chunks.shape[1]), jnp.bfloat16),
        interpret=interpret,
    )(jnp.asarray(bit_reversed_eye(n)), gram_rows, chunks)


def gram_adasum(grad_pair):
    devices = lax.axis_size("dp")
    me = lax.axis_index("dp")
    flat = grad_pair.reshape(devices, -1)
    chunks = lax.all_to_all(flat, "dp", 0, 0, tiled=True)
    tensors = grad_pair.shape[0]
    per_tensor = devices // tensors
    mine = me // per_tensor
    partial = jnp.dot(chunks, chunks.T, precision=HIGH, preferred_element_type=jnp.float32)
    rows = lax.all_to_all(partial[:, None, :], "dp", 0, 0, tiled=True)
    rows = jnp.sum(rows.reshape(tensors, per_tensor, partial.shape[1]), axis=1)
    spread = jnp.broadcast_to(rows.reshape(1, -1), (devices, tensors * partial.shape[1]))
    gram_rows = lax.all_to_all(spread, "dp", 0, 0, tiled=True)
    return combine(gram_rows, chunks)


def per_device(activations, upstream, section_norm_gain, adapter_down_weight, adapter_up_weight):
    passed_local, grad_pair = replica_backward(
        activations[0],
        upstream[0],
        section_norm_gain[0],
        adapter_down_weight[0],
        adapter_up_weight[0],
    )
    shifted = from_behind(passed_local[None], "section", -1)
    merged_gradient = gram_adasum(grad_pair)
    return (shifted, merged_gradient)


def solution(mesh):
    return jax.shard_map(
        per_device,
        mesh=mesh,
        in_specs=(
            P("section", "dp", None),
            P("section", "dp", None),
            P("section", None),
            P("section", None, None),
            P("section", None, None),
        ),
        out_specs=(P("section", "dp", None), P("section", "dp")),
        check_vma=False,
    )
```

```python
import numpy as np
import jax
import jax.numpy as jnp
from jax import lax
from jax.sharding import PartitionSpec as P
from jax.experimental import pallas as pl

norm_eps = 1e-05
pair_eps = 1e-06
adapter_scale = 2.0
HIGH = lax.Precision.HIGHEST


def swapped(value, axis, bit):
    mask = 2**bit
    pairs = [(source, source ^ mask) for source in range(lax.axis_size(axis))]
    return lax.ppermute(value, axis, pairs)


def from_behind(x, axis, by):
    size = lax.axis_size(axis)
    pairs = [(i, i + by) for i in range(size) if 0 <= i + by < size]
    return lax.ppermute(x, axis, pairs)


def replica_backward(inputs, incoming_gradient, gain_row, down_rows, upward_rows):
    widened = inputs.astype(jnp.float32)
    inverse = lax.rsqrt(jnp.mean(widened * widened, axis=-1, keepdims=True) + norm_eps)
    scaled = widened * inverse
    normed = (scaled * gain_row).astype(jnp.bfloat16)
    reduced_gradient = jnp.einsum(
        "sh,gh->sg", normed, down_rows, preferred_element_type=jnp.float32
    ).astype(jnp.bfloat16)
    count_of_rows = inputs.shape[0]
    upward_term = (
        adapter_scale
        * jnp.einsum(
            "tk,td->kd", reduced_gradient, incoming_gradient, preferred_element_type=jnp.float32
        )
        / count_of_rows
    )
    backward_lowrank = (
        adapter_scale
        * jnp.einsum(
            "sh,gh->sg", incoming_gradient, upward_rows, preferred_element_type=jnp.float32
        )
    ).astype(jnp.bfloat16)
    down_term = (
        jnp.einsum("tk,td->kd", backward_lowrank, normed, preferred_element_type=jnp.float32)
        / count_of_rows
    )
    back_norm = (
        jnp.einsum("tk,kd->td", backward_lowrank, down_rows, preferred_element_type=jnp.float32)
        * gain_row
    )
    centre = jnp.mean(back_norm * scaled, axis=-1, keepdims=True)
    passed = incoming_gradient.astype(jnp.float32) + inverse * (back_norm - scaled * centre)
    return (passed.astype(jnp.bfloat16), jnp.stack([down_term, upward_term]))


def swap_rows(c, level_bit):
    t, n = c.shape[0], c.shape[1]
    rest = c.shape[2:]
    g = c.reshape((t, n // 2 ** (level_bit + 1), 2, 2 ** level_bit) + rest)
    return g[:, :, ::-1].reshape(c.shape)


def coefficient_tree(gram):
    tensors, n = gram.shape[0], gram.shape[1]
    coef = jnp.broadcast_to(jnp.eye(n, dtype=jnp.float32), (tensors, n, n))
    for level_bit in range(n.bit_length() - 1):
        partner = swap_rows(coef, level_bit)
        gc = jnp.einsum("tra,tab->trb", coef, gram, precision=HIGH)
        inner_sum = jnp.sum(gc * partner, axis=-1, keepdims=True)
        own_square = jnp.sum(gc * coef, axis=-1, keepdims=True)
        far_square = swap_rows(own_square, level_bit)
        keep_coef = 1.0 - inner_sum / (2.0 * (own_square + pair_eps))
        take_coef = 1.0 - inner_sum / (2.0 * (far_square + pair_eps))
        coef = keep_coef * coef + take_coef * partner
    return coef[:, 0, :]


def bit_reversed_eye(n):
    bits = n.bit_length() - 1
    order = [int(format(i, f"0{bits}b")[::-1], 2) for i in range(n)]
    return np.eye(n, dtype=np.float32)[order]


def combine_kernel(gram_ref, chunks_ref, out_ref):
    n = gram_ref.shape[0]
    first_tensor = lax.axis_index("dp") < lax.axis_size("dp") // 2
    gram = jnp.where(first_tensor, gram_ref[:, 0:n], gram_ref[:, n:2 * n])
    rows = lax.broadcasted_iota(jnp.int32, (n, n), 0)
    cols = lax.broadcasted_iota(jnp.int32, (n, n), 1)
    bits = n.bit_length() - 1
    reversed_rows = jnp.zeros_like(rows)
    for b in range(bits):
        reversed_rows = reversed_rows + ((rows >> b) & 1) * (1 << (bits - 1 - b))
    coef = (cols == reversed_rows).astype(jnp.float32)
    while coef.shape[0] > 1:
        half = coef.shape[0] // 2
        first, second = coef[:half], coef[half:]
        g_first = jnp.dot(first, gram, precision=HIGH, preferred_element_type=jnp.float32)
        g_second = jnp.dot(second, gram, precision=HIGH, preferred_element_type=jnp.float32)
        inner_sum = jnp.sum(g_first * second, axis=1, keepdims=True)
        own_square = jnp.sum(g_first * first, axis=1, keepdims=True)
        far_square = jnp.sum(g_second * second, axis=1, keepdims=True)
        keep_coef = 1.0 - inner_sum / (2.0 * (own_square + pair_eps))
        take_coef = 1.0 - inner_sum / (2.0 * (far_square + pair_eps))
        coef = keep_coef * first + take_coef * second
    eye = (rows == cols).astype(jnp.float32)
    column = lax.dot_general(
        eye, coef, (((1,), (1,)), ((), ())), precision=HIGH, preferred_element_type=jnp.float32
    )
    combined = jnp.sum(column * chunks_ref[...], axis=0, keepdims=True)
    out_ref[...] = combined.astype(out_ref.dtype)


def combine(gram_rows, chunks, interpret=False):
    n = gram_rows.shape[0]
    return pl.pallas_call(
        combine_kernel,
        out_shape=jax.ShapeDtypeStruct((1, chunks.shape[1]), jnp.bfloat16),
        interpret=interpret,
    )(gram_rows, chunks)


def gram_adasum(grad_pair, passed):
    devices = lax.axis_size("dp")
    me = lax.axis_index("dp")
    flat = grad_pair.reshape(devices, -1)
    chunks = lax.all_to_all(flat, "dp", 0, 0, tiled=True)
    tensors = grad_pair.shape[0]
    per_tensor = devices // tensors
    mine = me // per_tensor
    partial = jnp.dot(chunks, chunks.T, precision=HIGH, preferred_element_type=jnp.float32)
    rows = lax.all_to_all(partial[:, None, :], "dp", 0, 0, tiled=True)
    rows = jnp.sum(rows.reshape(tensors, per_tensor, partial.shape[1]), axis=1)
    spread = jnp.broadcast_to(rows.reshape(1, -1), (devices, tensors * partial.shape[1]))
    spread, passed = lax.optimization_barrier((spread, passed))
    has_next = lax.axis_index("section") < lax.axis_size("section") - 1
    passed = jnp.where(has_next, passed, jnp.zeros_like(passed))
    gram_rows = lax.all_to_all(spread, "dp", 0, 0, tiled=True)
    return combine(gram_rows, chunks), passed


def per_device(activations, upstream, section_norm_gain, adapter_down_weight, adapter_up_weight):
    passed_local, grad_pair = replica_backward(
        activations[0],
        upstream[0],
        section_norm_gain[0],
        adapter_down_weight[0],
        adapter_up_weight[0],
    )
    shifted = from_behind(passed_local[None], "section", -1)
    merged_gradient, shifted = gram_adasum(grad_pair, shifted)
    return (shifted, merged_gradient)


def solution(mesh):
    return jax.shard_map(
        per_device,
        mesh=mesh,
        in_specs=(
            P("section", "dp", None),
            P("section", "dp", None),
            P("section", None),
            P("section", None, None),
            P("section", None, None),
        ),
        out_specs=(P("section", "dp", None), P("section", "dp")),
        check_vma=False,
    )
```

```python
import numpy as np
import jax
import jax.numpy as jnp
from jax import lax
from jax.sharding import PartitionSpec as P
from jax.experimental import pallas as pl
from jax.experimental.pallas import tpu as pltpu

norm_eps = 1e-05
pair_eps = 1e-06
adapter_scale = 2.0
HIGH = lax.Precision.HIGHEST


def swapped(value, axis, bit):
    mask = 2**bit
    pairs = [(source, source ^ mask) for source in range(lax.axis_size(axis))]
    return lax.ppermute(value, axis, pairs)


def from_behind(x, axis, by):
    size = lax.axis_size(axis)
    pairs = [(i, i + by) for i in range(size) if 0 <= i + by < size]
    return lax.ppermute(x, axis, pairs)


def replica_backward(inputs, incoming_gradient, gain_row, down_rows, upward_rows):
    widened = inputs.astype(jnp.float32)
    inverse = lax.rsqrt(jnp.mean(widened * widened, axis=-1, keepdims=True) + norm_eps)
    scaled = widened * inverse
    normed = (scaled * gain_row).astype(jnp.bfloat16)
    reduced_gradient = jnp.einsum(
        "sh,gh->sg", normed, down_rows, preferred_element_type=jnp.float32
    ).astype(jnp.bfloat16)
    count_of_rows = inputs.shape[0]
    upward_term = (
        adapter_scale
        * jnp.einsum(
            "tk,td->kd", reduced_gradient, incoming_gradient, preferred_element_type=jnp.float32
        )
        / count_of_rows
    )
    backward_lowrank = (
        adapter_scale
        * jnp.einsum(
            "sh,gh->sg", incoming_gradient, upward_rows, preferred_element_type=jnp.float32
        )
    ).astype(jnp.bfloat16)
    down_term = (
        jnp.einsum("tk,td->kd", backward_lowrank, normed, preferred_element_type=jnp.float32)
        / count_of_rows
    )
    back_norm = (
        jnp.einsum("tk,kd->td", backward_lowrank, down_rows, preferred_element_type=jnp.float32)
        * gain_row
    )
    centre = jnp.mean(back_norm * scaled, axis=-1, keepdims=True)
    passed = incoming_gradient.astype(jnp.float32) + inverse * (back_norm - scaled * centre)
    return (passed.astype(jnp.bfloat16), jnp.stack([down_term, upward_term]))


def swap_rows(c, level_bit):
    t, n = c.shape[0], c.shape[1]
    rest = c.shape[2:]
    g = c.reshape((t, n // 2 ** (level_bit + 1), 2, 2 ** level_bit) + rest)
    return g[:, :, ::-1].reshape(c.shape)


def coefficient_tree(gram):
    tensors, n = gram.shape[0], gram.shape[1]
    coef = jnp.broadcast_to(jnp.eye(n, dtype=jnp.float32), (tensors, n, n))
    for level_bit in range(n.bit_length() - 1):
        partner = swap_rows(coef, level_bit)
        gc = jnp.einsum("tra,tab->trb", coef, gram, precision=HIGH)
        inner_sum = jnp.sum(gc * partner, axis=-1, keepdims=True)
        own_square = jnp.sum(gc * coef, axis=-1, keepdims=True)
        far_square = swap_rows(own_square, level_bit)
        keep_coef = 1.0 - inner_sum / (2.0 * (own_square + pair_eps))
        take_coef = 1.0 - inner_sum / (2.0 * (far_square + pair_eps))
        coef = keep_coef * coef + take_coef * partner
    return coef[:, 0, :]


def bit_reversed_eye(n):
    bits = n.bit_length() - 1
    order = [int(format(i, f"0{bits}b")[::-1], 2) for i in range(n)]
    return np.eye(n, dtype=np.float32)[order]


def combine_kernel(gram_ref, chunks_hbm, out_ref, chunks_ref, copy_sem):
    fetch = pltpu.make_async_copy(chunks_hbm, chunks_ref, copy_sem)
    fetch.start()
    n = gram_ref.shape[0]
    first_tensor = lax.axis_index("dp") < lax.axis_size("dp") // 2
    gram = jnp.where(first_tensor, gram_ref[:, 0:n], gram_ref[:, n:2 * n])
    rows = lax.broadcasted_iota(jnp.int32, (n, n), 0)
    cols = lax.broadcasted_iota(jnp.int32, (n, n), 1)
    bits = n.bit_length() - 1
    reversed_rows = jnp.zeros_like(rows)
    for b in range(bits):
        reversed_rows = reversed_rows + ((rows >> b) & 1) * (1 << (bits - 1 - b))
    coef = (cols == reversed_rows).astype(jnp.float32)
    while coef.shape[0] > 1:
        half = coef.shape[0] // 2
        first, second = coef[:half], coef[half:]
        g_first = jnp.dot(first, gram, precision=HIGH, preferred_element_type=jnp.float32)
        g_second = jnp.dot(second, gram, precision=HIGH, preferred_element_type=jnp.float32)
        inner_sum = jnp.sum(g_first * second, axis=1, keepdims=True)
        own_square = jnp.sum(g_first * first, axis=1, keepdims=True)
        far_square = jnp.sum(g_second * second, axis=1, keepdims=True)
        keep_coef = 1.0 - inner_sum / (2.0 * (own_square + pair_eps))
        take_coef = 1.0 - inner_sum / (2.0 * (far_square + pair_eps))
        coef = keep_coef * first + take_coef * second
    eye = (rows == cols).astype(jnp.float32)
    column = lax.dot_general(
        eye, coef, (((1,), (1,)), ((), ())), precision=HIGH, preferred_element_type=jnp.float32
    )
    fetch.wait()
    combined = jnp.sum(column * chunks_ref[...], axis=0, keepdims=True)
    out_ref[...] = combined.astype(out_ref.dtype)


def combine(gram_rows, chunks, interpret=False):
    n = gram_rows.shape[0]
    return pl.pallas_call(
        combine_kernel,
        out_shape=jax.ShapeDtypeStruct((1, chunks.shape[1]), jnp.bfloat16),
        in_specs=[
            pl.BlockSpec(memory_space=pltpu.VMEM),
            pl.BlockSpec(memory_space=pl.ANY),
        ],
        out_specs=pl.BlockSpec(memory_space=pltpu.VMEM),
        scratch_shapes=[pltpu.VMEM(chunks.shape, chunks.dtype), pltpu.SemaphoreType.DMA],
        interpret=interpret,
    )(gram_rows, chunks)


def gram_adasum(grad_pair):
    devices = lax.axis_size("dp")
    me = lax.axis_index("dp")
    flat = grad_pair.reshape(devices, -1)
    chunks = lax.all_to_all(flat, "dp", 0, 0, tiled=True)
    tensors = grad_pair.shape[0]
    per_tensor = devices // tensors
    mine = me // per_tensor
    partial = jnp.dot(chunks, chunks.T, precision=HIGH, preferred_element_type=jnp.float32)
    rows = lax.all_to_all(partial[:, None, :], "dp", 0, 0, tiled=True)
    rows = jnp.sum(rows.reshape(tensors, per_tensor, partial.shape[1]), axis=1)
    spread = jnp.broadcast_to(rows.reshape(1, -1), (devices, tensors * partial.shape[1]))
    gram_rows = lax.all_to_all(spread, "dp", 0, 0, tiled=True)
    return combine(gram_rows, chunks)


def per_device(activations, upstream, section_norm_gain, adapter_down_weight, adapter_up_weight):
    passed_local, grad_pair = replica_backward(
        activations[0],
        upstream[0],
        section_norm_gain[0],
        adapter_down_weight[0],
        adapter_up_weight[0],
    )
    shifted = from_behind(passed_local[None], "section", -1)
    merged_gradient = gram_adasum(grad_pair)
    return (shifted, merged_gradient)


def solution(mesh):
    return jax.shard_map(
        per_device,
        mesh=mesh,
        in_specs=(
            P("section", "dp", None),
            P("section", "dp", None),
            P("section", None),
            P("section", None, None),
            P("section", None, None),
        ),
        out_specs=(P("section", "dp", None), P("section", "dp")),
        check_vma=False,
    )
```

```python
import numpy as np
import jax
import jax.numpy as jnp
from jax import lax
from jax.sharding import PartitionSpec as P
from jax.experimental import pallas as pl

norm_eps = 1e-05
pair_eps = 1e-06
adapter_scale = 2.0
HIGH = lax.Precision.HIGHEST


def swapped(value, axis, bit):
    mask = 2**bit
    pairs = [(source, source ^ mask) for source in range(lax.axis_size(axis))]
    return lax.ppermute(value, axis, pairs)


def from_behind(x, axis, by):
    size = lax.axis_size(axis)
    pairs = [(i, i + by) for i in range(size) if 0 <= i + by < size]
    return lax.ppermute(x, axis, pairs)


def replica_backward(inputs, incoming_gradient, gain_row, down_rows, upward_rows):
    widened = inputs.astype(jnp.float32)
    inverse = lax.rsqrt(jnp.mean(widened * widened, axis=-1, keepdims=True) + norm_eps)
    scaled = widened * inverse
    normed = (scaled * gain_row).astype(jnp.bfloat16)
    reduced_gradient = jnp.einsum(
        "sh,gh->sg", normed, down_rows, preferred_element_type=jnp.float32
    ).astype(jnp.bfloat16)
    count_of_rows = inputs.shape[0]
    upward_term = (
        adapter_scale
        * jnp.einsum(
            "tk,td->kd", reduced_gradient, incoming_gradient, preferred_element_type=jnp.float32
        )
        / count_of_rows
    )
    backward_lowrank = (
        adapter_scale
        * jnp.einsum(
            "sh,gh->sg", incoming_gradient, upward_rows, preferred_element_type=jnp.float32
        )
    ).astype(jnp.bfloat16)
    down_term = (
        jnp.einsum("tk,td->kd", backward_lowrank, normed, preferred_element_type=jnp.float32)
        / count_of_rows
    )
    back_norm = (
        jnp.einsum("tk,kd->td", backward_lowrank, down_rows, preferred_element_type=jnp.float32)
        * gain_row
    )
    centre = jnp.mean(back_norm * scaled, axis=-1, keepdims=True)
    passed = incoming_gradient.astype(jnp.float32) + inverse * (back_norm - scaled * centre)
    return (passed.astype(jnp.bfloat16), jnp.stack([down_term, upward_term]))


def swap_rows(c, level_bit):
    t, n = c.shape[0], c.shape[1]
    rest = c.shape[2:]
    g = c.reshape((t, n // 2 ** (level_bit + 1), 2, 2 ** level_bit) + rest)
    return g[:, :, ::-1].reshape(c.shape)


def coefficient_tree(gram):
    tensors, n = gram.shape[0], gram.shape[1]
    coef = jnp.broadcast_to(jnp.eye(n, dtype=jnp.float32), (tensors, n, n))
    for level_bit in range(n.bit_length() - 1):
        partner = swap_rows(coef, level_bit)
        gc = jnp.einsum("tra,tab->trb", coef, gram, precision=HIGH)
        inner_sum = jnp.sum(gc * partner, axis=-1, keepdims=True)
        own_square = jnp.sum(gc * coef, axis=-1, keepdims=True)
        far_square = swap_rows(own_square, level_bit)
        keep_coef = 1.0 - inner_sum / (2.0 * (own_square + pair_eps))
        take_coef = 1.0 - inner_sum / (2.0 * (far_square + pair_eps))
        coef = keep_coef * coef + take_coef * partner
    return coef[:, 0, :]


def bit_reversed_eye(n):
    bits = n.bit_length() - 1
    order = [int(format(i, f"0{bits}b")[::-1], 2) for i in range(n)]
    return np.eye(n, dtype=np.float32)[order]


def combine_kernel(start_ref, gram_ref, chunks_ref, out_ref):
    n = gram_ref.shape[0]
    first_tensor = lax.axis_index("dp") < lax.axis_size("dp") // 2
    gram = jnp.where(first_tensor, gram_ref[:, 0:n], gram_ref[:, n:2 * n])
    coef = start_ref[...]
    while coef.shape[0] > 1:
        half = coef.shape[0] // 2
        first, second = coef[:half], coef[half:]
        g_both = jnp.dot(coef, gram, precision=HIGH, preferred_element_type=jnp.float32)
        g_first, g_second = g_both[:half], g_both[half:]
        inner_sum = jnp.sum(g_first * second, axis=1, keepdims=True)
        own_square = jnp.sum(g_first * first, axis=1, keepdims=True)
        far_square = jnp.sum(g_second * second, axis=1, keepdims=True)
        keep_coef = 1.0 - inner_sum / (2.0 * (own_square + pair_eps))
        take_coef = 1.0 - inner_sum / (2.0 * (far_square + pair_eps))
        coef = keep_coef * first + take_coef * second
    eye = (
        lax.broadcasted_iota(jnp.int32, (n, n), 0) == lax.broadcasted_iota(jnp.int32, (n, n), 1)
    ).astype(jnp.float32)
    column = lax.dot_general(
        eye, coef, (((1,), (1,)), ((), ())), precision=HIGH, preferred_element_type=jnp.float32
    )
    combined = jnp.sum(column * chunks_ref[...], axis=0, keepdims=True)
    out_ref[...] = combined.astype(out_ref.dtype)


def combine(gram_rows, chunks, interpret=False):
    n = gram_rows.shape[0]
    return pl.pallas_call(
        combine_kernel,
        out_shape=jax.ShapeDtypeStruct((1, chunks.shape[1]), jnp.bfloat16),
        interpret=interpret,
    )(jnp.asarray(bit_reversed_eye(n)), gram_rows, chunks)


def gram_adasum(grad_pair):
    devices = lax.axis_size("dp")
    me = lax.axis_index("dp")
    flat = grad_pair.reshape(devices, -1)
    chunks = lax.all_to_all(flat, "dp", 0, 0, tiled=True)
    tensors = grad_pair.shape[0]
    per_tensor = devices // tensors
    mine = me // per_tensor
    partial = jnp.dot(chunks, chunks.T, precision=HIGH, preferred_element_type=jnp.float32)
    rows = lax.all_to_all(partial[:, None, :], "dp", 0, 0, tiled=True)
    rows = jnp.sum(rows.reshape(tensors, per_tensor, partial.shape[1]), axis=1)
    spread = jnp.broadcast_to(rows.reshape(1, -1), (devices, tensors * partial.shape[1]))
    gram_rows = lax.all_to_all(spread, "dp", 0, 0, tiled=True)
    return combine(gram_rows, chunks)


def per_device(activations, upstream, section_norm_gain, adapter_down_weight, adapter_up_weight):
    passed_local, grad_pair = replica_backward(
        activations[0],
        upstream[0],
        section_norm_gain[0],
        adapter_down_weight[0],
        adapter_up_weight[0],
    )
    shifted = from_behind(passed_local[None], "section", -1)
    merged_gradient = gram_adasum(grad_pair)
    return (shifted, merged_gradient)


def solution(mesh):
    return jax.shard_map(
        per_device,
        mesh=mesh,
        in_specs=(
            P("section", "dp", None),
            P("section", "dp", None),
            P("section", None),
            P("section", None, None),
            P("section", None, None),
        ),
        out_specs=(P("section", "dp", None), P("section", "dp")),
        check_vma=False,
    )
```
